128 devices in a mesh: node: 4 (over x), ep: 32 (over y, z, core).
Axes of the slice: x: 4, y: 4, z: 4, core: 2. Of those that a mesh axis runs over, the one named last changes fastest.
Arguments:
- images: bfloat16 [128, 257, 1280], P(('node', 'ep')), may hold values from -6 to 6
- w_query: bfloat16 [1280, 1280], P(None, 'node'), may hold values from -6 to 6
- w_key: bfloat16 [1280, 1280], P(None, 'node'), may hold values from -6 to 6
- w_value: bfloat16 [1280, 1280], P(None, 'node'), may hold values from -0.15625 to 0.15625
- w_output: bfloat16 [1280, 1280], replicated, may hold values from -0.15625 to 0.15625
- router: bfloat16 [1280, 32], replicated, may hold values from -0.15625 to 0.15625
- w_in: bfloat16 [32, 1280, 5120], P('ep', None, 'node'), may hold values from -0.15625 to 0.15625
- w_out: bfloat16 [32, 5120, 1280], P('ep', 'node'), may hold values from -0.078125 to 0.078125
- routes: int32 [128, 257, 2], P(('node', 'ep')), may hold values from 0 to 31, all different within a row; in each aligned block of 257 rows (0 to 256, 257 to 513, ..., all dimensions but the last counted through in order) at most 24 rows name the same one
Outputs:
- output: bfloat16 [128, 257, 1280], P(('node', 'ep'))
The draws below stay inside these ranges and needn't reach their ends.
Inputs may be any that keep to these rules, and one draw needn't show every extreme that they name: `routes`: the two experts of a token differ. At most 24 tokens of one image name the same expert, and in every draw some image has an expert named by exactly 24 of its tokens.
All inputs are finite; a program needn't handle non-finite values.
Results may differ from the reference program's by a relative error of at most 0.0085.
Values may be sent and summed in bfloat16 or wider, within the bound.
No kernel may reach another device: no remote copies, remote signals or barrier semaphores. Data moves between devices by JAX's collectives and lax.ppermute only.
A program may use at most 128 MiB of HBM per device.

```python
import math
import jax
import jax.numpy as jnp
import numpy as np
from jax import lax

D = 1280
HEADS = 16
FF = 5120
TOK = 257
CAP = 24
EXPERTS = 32
IMAGES = 128
N_NODE = 4


def attention_pair(key):
    first_base = jnp.clip(jax.random.normal(jax.random.fold_in(key, 11), (D, D), jnp.float32), -4.0, 4.0)
    second_base = jnp.clip(jax.random.normal(jax.random.fold_in(key, 12), (D, D), jnp.float32), -4.0, 4.0)
    return (first_base, second_base)


def draw_w_query(key, part):
    first_base, second_base = attention_pair(key)
    values = first_base * D ** (-0.5)
    return values.astype(jnp.bfloat16)


def draw_w_key(key, part):
    first_base, second_base = attention_pair(key)
    values = second_base * D ** (-0.5)
    return values.astype(jnp.bfloat16)


def draw_images(key, part):
    shape = (IMAGES, TOK, D)
    values = jnp.clip(jax.random.normal(jax.random.fold_in(key, 23), shape, jnp.float32), -6.0, 6.0)
    return values.astype(jnp.bfloat16)


def levels(own_key, extent, shards, low, top_value):
    loudness, own = 1.0, jax.random.fold_in(own_key, 6)
    for axis_at, blocks in shards:
        heights = jnp.exp(jax.random.uniform(jax.random.fold_in(own, axis_at), (blocks,), jnp.float32, low / len(shards), top_value / len(shards)))
        loudness = loudness * jnp.repeat(heights, extent[axis_at] // blocks).reshape([-1 if axis == axis_at else 1 for axis in range(len(extent))])
    return loudness


def assign_block(key, own, number, rows, count, top, limit, lean):
    order = jax.random.permutation(key, count)
    heavy_load, common = portions_of(count, rows * top, limit, lean, True), portions_of(count, rows * top, limit, lean, False)
    places = jnp.arange(count)

    def named(tallies, turn):
        used = int((tallies > 0).sum())
        fixed = max(1, used // 4)
        passed = fixed + (places - fixed + turn * (used - fixed)) % max(1, count - fixed)
        return jnp.zeros((count,), jnp.int32).at[order[jnp.where(places < fixed, places, passed)]].set(jnp.asarray(tallies, jnp.int32))

    tallies = jnp.where(number % 4 == 0, named(heavy_load, number // 4), named(common, number - number // 4 - 1))
    mixed = jax.random.permutation(jax.random.fold_in(own, 3), count)
    donor, receiver = mixed[0:count // 2 * 2:2], mixed[1:count // 2 * 2:2]
    slack = jnp.minimum(tallies[donor] - 1, limit - tallies[receiver]) // 2
    slack = jnp.where((donor == order[0]) | (receiver == order[0]) | (tallies[receiver] == 0), 0, jnp.maximum(slack, 0))
    passed = jax.random.randint(jax.random.fold_in(own, 4), (count // 2,), 0, 1 << 20) % (slack + 1)
    tallies = tallies.at[donor].add(-passed).at[receiver].add(passed)
    labels = jnp.searchsorted(jnp.cumsum(tallies), jnp.arange(rows * top), side="right").astype(jnp.int32)
    grid = labels.reshape(top, rows).T
    grid = grid[jax.random.permutation(jax.random.fold_in(own, 1), rows)]
    turn = jax.random.randint(jax.random.fold_in(own, 2), (rows, 1), 0, top)
    return jnp.take_along_axis(grid, (jnp.arange(top)[None, :] + turn) % top, axis=1)


def portions_of(amount, total, most, lean, full):
    weights = [(1 << 20) // math.isqrt(grade ** lean) + 1 for grade in range(1, amount + 1)]
    largest = most if full else min(most, max(-(-total // amount), total * weights[0] // sum(weights)))
    least = 1 if total - largest >= amount - 1 else 0
    counts, surplus = [largest] + [least] * (amount - 1), total - largest - least * (amount - 1)
    while surplus > 0:
        candidates = [i for i in range(1, amount) if counts[i] < largest] or [i for i in range(1, amount) if counts[i] < most]
        pool, left = sum([weights[i] for i in candidates]), surplus
        for i in candidates:
            more = min(most - counts[i], max(1, left * weights[i] // pool), surplus)
            counts[i] = counts[i] + more
            surplus = surplus - more
    return np.array(counts)


def bell_draw(stream_key, shape, scale, limit, cuts=(), held_as=jnp.bfloat16):
    array = jax.random.normal(stream_key, shape, jnp.float32) * scale
    if len(cuts) > 0:
        array = levels(stream_key, shape, cuts, -0.22, 0.18) * array
    return jnp.clip(array, min=-limit, max=limit).astype(held_as)


def setup_inputs(seed: int = 0) -> dict:
    keys = jax.random.split(jax.random.key(seed), 10)
    images = draw_images(jax.random.fold_in(keys[9], 71), 0)
    w_query = draw_w_query(jax.random.fold_in(keys[9], 71), 0)
    w_key = draw_w_key(jax.random.fold_in(keys[9], 71), 0)
    w_value = bell_draw(keys[3], (D, D), D ** -0.5, 0.15625, ((1, 4),))
    w_output = bell_draw(keys[4], (D, D), D ** -0.5, 0.15625)
    router = bell_draw(keys[5], (D, EXPERTS), D ** -0.5, 0.15625)
    w_in = bell_draw(keys[6], (EXPERTS, D, FF), D ** -0.5, 0.15625, ((0, 32), (2, 4)))
    w_out = bell_draw(keys[7], (EXPERTS, FF, D), FF ** -0.5, 0.078125, ((0, 32), (1, 4)))
    routes_keys = jax.random.split(jax.random.fold_in(keys[8], 1), IMAGES * TOK // TOK)
    routes_turns = jax.random.permutation(jax.random.fold_in(keys[8], 3), IMAGES * TOK // TOK)
    routes = jax.vmap(lambda own, number: assign_block(jax.random.fold_in(keys[8], 2), own, number, TOK, EXPERTS, 2, CAP, 2))(routes_keys, routes_turns).reshape((IMAGES, TOK, 2))
    return dict(images=images, w_query=w_query, w_key=w_key, w_value=w_value, w_output=w_output, router=router, w_in=w_in, w_out=w_out, routes=routes)


def layer_norm(values):
    center = values - lax.optimization_barrier(jnp.mean(values, axis=-1, keepdims=True))
    spread = lax.optimization_barrier(jnp.mean(center * center, axis=-1, keepdims=True))
    return center * lax.rsqrt(spread + 1e-06)

def slot_table(chosen, num_experts):
    onehot = (chosen[..., None] == jnp.arange(num_experts, dtype=jnp.int32)).astype(jnp.int32)
    before = jnp.cumsum(onehot, axis=1) - onehot
    return lax.optimization_barrier(jnp.sum(before * onehot, axis=-1)).astype(jnp.int32)

def reference(images, w_query, w_key, w_value, w_output, router, w_in, w_out, routes):
    head_size = D // HEADS

    def attend_image(single):
        inputs = single.astype(jnp.float32)
        normed = layer_norm(inputs).astype(jnp.bfloat16)
        queries = jnp.dot(normed, w_query, preferred_element_type=jnp.float32).astype(jnp.bfloat16)
        projected_keys = jnp.dot(normed, w_key, preferred_element_type=jnp.float32).astype(jnp.bfloat16)
        projected_values = jnp.dot(normed, w_value, preferred_element_type=jnp.float32).astype(jnp.bfloat16)
        query_heads = queries.astype(jnp.float32).reshape(TOK, HEADS, head_size)
        key_heads = projected_keys.astype(jnp.float32).reshape(TOK, HEADS, head_size)
        value_heads = projected_values.astype(jnp.float32).reshape(TOK, HEADS, head_size)
        scores = jnp.einsum('qhd,khd->hqk', query_heads, key_heads) / math.sqrt(head_size)
        weights = jax.nn.softmax(scores, axis=-1).astype(jnp.bfloat16)
        mixture = jnp.einsum('hqk,khd->qhd', weights.astype(jnp.float32), value_heads)
        mixture = mixture.astype(jnp.bfloat16).reshape(TOK, D)
        return inputs + jnp.dot(mixture, w_output, preferred_element_type=jnp.float32)
    middle = lax.map(attend_image, images)
    normed = layer_norm(middle).astype(jnp.bfloat16)
    logits = jnp.einsum('itd,de->ite', normed.astype(jnp.float32), router.astype(jnp.float32))
    chosen_mask = routes[..., None] == jnp.arange(EXPERTS, dtype=jnp.int32)
    chosen_logit = lax.optimization_barrier(jnp.sum(jnp.where(chosen_mask, logits[:, :, None, :], jnp.float32(0.0)), axis=-1))
    gate_values = jax.nn.sigmoid(chosen_logit)
    flat_routes = routes.reshape(IMAGES, 2 * TOK)
    slot_index = slot_table(flat_routes, EXPERTS)
    per_expert = IMAGES * CAP
    image_base = jnp.arange(IMAGES, dtype=jnp.int32)[:, None] * CAP
    position = (flat_routes * per_expert + image_base + slot_index).reshape(-1).astype(jnp.int32)
    token_ids = jnp.arange(IMAGES * 2 * TOK, dtype=jnp.int32) // 2
    source = jnp.full((EXPERTS * per_expert,), -1, jnp.int32).at[position].set(token_ids)
    token_rows = normed.reshape(IMAGES * TOK, D)
    gathered = jnp.take(token_rows, jnp.maximum(source, 0), axis=0)
    gathered = jnp.where(source[:, None] >= 0, gathered, jnp.zeros_like(gathered))
    gathered = gathered.reshape(EXPERTS, per_expert, D)
    quarter = FF // N_NODE

    def run_expert(operands):
        buffer, first_weight, second_weight = operands
        summed = jnp.zeros((per_expert, D), jnp.float32)
        for section in range(N_NODE):
            pre_act = jnp.dot(buffer, first_weight[:, section * quarter:(section + 1) * quarter], preferred_element_type=jnp.float32)
            hidden = jax.nn.gelu(pre_act, approximate=True).astype(jnp.bfloat16)
            partial_sum = jnp.dot(hidden, second_weight[section * quarter:(section + 1) * quarter, :], preferred_element_type=jnp.float32).astype(jnp.bfloat16)
            summed = summed + lax.optimization_barrier(partial_sum).astype(jnp.float32)
        return summed.astype(jnp.bfloat16)
    results = lax.map(run_expert, (gathered, w_in, w_out))
    picked = jnp.take(results.reshape(EXPERTS * per_expert, D), position, axis=0).reshape(IMAGES, TOK, 2, D)
    expert_mix = lax.optimization_barrier(jnp.sum(gate_values[..., None] * picked.astype(jnp.float32), axis=2))
    return (middle + expert_mix).astype(jnp.bfloat16)
```

```python
import math

import jax
import jax.numpy as jnp
from jax import lax
from jax.sharding import PartitionSpec as P

D = 1280
HEADS = 16
CAP = 24


def layer_norm(values):
    center = values - jnp.mean(values, axis=-1, keepdims=True)
    spread = jnp.mean(center * center, axis=-1, keepdims=True)
    return center * lax.rsqrt(spread + 1e-06)


def slot_table(chosen, num_experts):
    onehot = (chosen[..., None] == jnp.arange(num_experts, dtype=jnp.int32)).astype(jnp.int32)
    before = jnp.cumsum(onehot, axis=1) - onehot
    return jnp.sum(before * onehot, axis=-1)


def shards(images, w_query, w_key, w_value, w_output, router, w_in, w_out, routes):
    local_images, tokens_dev, width = images.shape
    head_size = D // HEADS
    local_heads = w_query.shape[1] // head_size
    node_count = lax.axis_size("node")
    column_count = lax.axis_size("ep")
    num_experts = router.shape[1]
    local_experts = w_in.shape[0]
    slot_count = local_images * CAP
    inputs = images.astype(jnp.float32)
    normed = layer_norm(inputs).astype(jnp.bfloat16)
    shard_rows = lax.all_gather(normed, "node", axis=0, tiled=True)
    number = shard_rows.shape[0]
    queries = jnp.einsum(
        "ctd,de->cte", shard_rows, w_query, preferred_element_type=jnp.float32
    ).astype(jnp.bfloat16)
    projected_keys = jnp.einsum(
        "ctd,de->cte", shard_rows, w_key, preferred_element_type=jnp.float32
    ).astype(jnp.bfloat16)
    projected_values = jnp.einsum(
        "ctd,de->cte", shard_rows, w_value, preferred_element_type=jnp.float32
    ).astype(jnp.bfloat16)
    query_heads = queries.reshape(number, tokens_dev, local_heads, head_size)
    key_heads = projected_keys.reshape(number, tokens_dev, local_heads, head_size)
    value_heads = projected_values.reshape(number, tokens_dev, local_heads, head_size)
    scores = jnp.einsum(
        "cqhd,ckhd->chqk", query_heads, key_heads, preferred_element_type=jnp.float32
    ) / math.sqrt(head_size)
    weights = jax.nn.softmax(scores, axis=-1).astype(jnp.bfloat16)
    mixture = jnp.einsum(
        "chqk,ckhd->cqhd", weights, value_heads, preferred_element_type=jnp.float32
    ).astype(jnp.bfloat16)
    head_results = mixture.reshape(number, tokens_dev, local_heads * head_size)
    attention = jnp.einsum(
        "itd,de->ite",
        lax.all_to_all(head_results, "node", split_axis=0, concat_axis=2, tiled=True),
        w_output,
        preferred_element_type=jnp.float32,
    )
    middle = inputs + attention
    normed_second = layer_norm(middle).astype(jnp.bfloat16)
    logits = jnp.einsum("itd,de->ite", normed_second, router, preferred_element_type=jnp.float32)
    chosen_mask = routes[..., None] == jnp.arange(num_experts, dtype=jnp.int32)
    chosen_logit = jnp.sum(jnp.where(chosen_mask, logits[:, :, None, :], jnp.float32(0.0)), axis=-1)
    gate_values = jax.nn.sigmoid(chosen_logit)
    flat_routes = routes.reshape(local_images, 2 * tokens_dev)
    slot_index = slot_table(flat_routes, num_experts)
    image_base = jnp.arange(local_images, dtype=jnp.int32)[:, None] * CAP
    position = (flat_routes * slot_count + image_base + slot_index).reshape(-1)
    token_ids = jnp.arange(local_images * 2 * tokens_dev, dtype=jnp.int32) // 2
    source = jnp.full((num_experts * slot_count,), -1, jnp.int32).at[position].set(token_ids)
    token_rows = normed_second.reshape(local_images * tokens_dev, width)
    gathered = jnp.take(token_rows, jnp.maximum(source, 0), axis=0)
    gathered = jnp.where(source[:, None] >= 0, gathered, jnp.zeros_like(gathered))
    outgoing = gathered.reshape(column_count, local_experts, slot_count, width)
    by_column = lax.all_to_all(outgoing, "ep", split_axis=0, concat_axis=0, tiled=True)
    arrived = lax.all_gather(by_column, "node", axis=0, tiled=True)
    pre_act = jnp.einsum("lesd,edf->lesf", arrived, w_in, preferred_element_type=jnp.float32)
    hidden = jax.nn.gelu(pre_act, approximate=True).astype(jnp.bfloat16)
    partial_sum = jnp.einsum(
        "lesf,efd->lesd", hidden, w_out, preferred_element_type=jnp.float32
    ).astype(jnp.bfloat16)
    partial_sum = partial_sum.reshape(node_count * column_count * local_experts * slot_count, width)
    summed = lax.psum_scatter(partial_sum, "node", scatter_dimension=0, tiled=True)
    summed = summed.reshape(column_count, local_experts, slot_count, width)
    expert_result = lax.all_to_all(summed, "ep", split_axis=0, concat_axis=0, tiled=True)
    result_rows = expert_result.reshape(num_experts * slot_count, width)
    picked = jnp.take(result_rows, position, axis=0).reshape(local_images, tokens_dev, 2, width)
    expert_mix = jnp.sum(gate_values[..., None] * picked.astype(jnp.float32), axis=2)
    return (middle + expert_mix).astype(jnp.bfloat16)


def solution(mesh):
    placed = (
        P(("node", "ep"), None, None),
        P(None, "node"),
        P(None, "node"),
        P(None, "node"),
        P(),
        P(),
        P("ep", None, "node"),
        P("ep", "node", None),
        P(("node", "ep"), None, None),
    )
    return jax.shard_map(
        shards, mesh=mesh, in_specs=placed, out_specs=P(("node", "ep"), None, None), check_vma=False
    )
```

```python
import math

import jax
import jax.numpy as jnp
from jax import lax
from jax.sharding import PartitionSpec as P

D = 1280
HEADS = 16
CAP = 24
CHUNKS = 4


def layer_norm(values):
    center = values - jnp.mean(values, axis=-1, keepdims=True)
    spread = jnp.mean(center * center, axis=-1, keepdims=True)
    return center * lax.rsqrt(spread + 1e-06)


def slot_table(chosen, num_experts):
    onehot = (chosen[..., None] == jnp.arange(num_experts, dtype=jnp.int32)).astype(jnp.int32)
    before = jnp.cumsum(onehot, axis=1) - onehot
    return jnp.sum(before * onehot, axis=-1)


def shards(images, w_query, w_key, w_value, w_output, router, w_in, w_out, routes):
    local_images, tokens_dev, width = images.shape
    head_size = D // HEADS
    local_heads = w_query.shape[1] // head_size
    node_count = lax.axis_size("node")
    column_count = lax.axis_size("ep")
    num_experts = router.shape[1]
    local_experts = w_in.shape[0]
    slot_count = local_images * CAP
    inputs = images.astype(jnp.float32)
    normed = layer_norm(inputs).astype(jnp.bfloat16)
    shard_rows = lax.all_gather(normed, "node", axis=0, tiled=True)
    number = shard_rows.shape[0]
    queries = jnp.einsum(
        "ctd,de->cte", shard_rows, w_query, preferred_element_type=jnp.float32
    ).astype(jnp.bfloat16)
    projected_keys = jnp.einsum(
        "ctd,de->cte", shard_rows, w_key, preferred_element_type=jnp.float32
    ).astype(jnp.bfloat16)
    projected_values = jnp.einsum(
        "ctd,de->cte", shard_rows, w_value, preferred_element_type=jnp.float32
    ).astype(jnp.bfloat16)
    query_heads = queries.reshape(number, tokens_dev, local_heads, head_size)
    key_heads = projected_keys.reshape(number, tokens_dev, local_heads, head_size)
    value_heads = projected_values.reshape(number, tokens_dev, local_heads, head_size)
    scores = jnp.einsum(
        "cqhd,ckhd->chqk", query_heads, key_heads, preferred_element_type=jnp.float32
    ) / math.sqrt(head_size)
    weights = jax.nn.softmax(scores, axis=-1).astype(jnp.bfloat16)
    mixture = jnp.einsum(
        "chqk,ckhd->cqhd", weights, value_heads, preferred_element_type=jnp.float32
    ).astype(jnp.bfloat16)
    head_results = mixture.reshape(number, tokens_dev, local_heads * head_size)
    attention = jnp.einsum(
        "itd,de->ite",
        lax.all_to_all(head_results, "node", split_axis=0, concat_axis=2, tiled=True),
        w_output,
        preferred_element_type=jnp.float32,
    )
    middle = inputs + attention
    normed_second = layer_norm(middle).astype(jnp.bfloat16)
    logits = jnp.einsum("itd,de->ite", normed_second, router, preferred_element_type=jnp.float32)
    chosen_mask = routes[..., None] == jnp.arange(num_experts, dtype=jnp.int32)
    chosen_logit = jnp.sum(jnp.where(chosen_mask, logits[:, :, None, :], jnp.float32(0.0)), axis=-1)
    gate_values = jax.nn.sigmoid(chosen_logit)
    flat_routes = routes.reshape(local_images, 2 * tokens_dev)
    slot_index = slot_table(flat_routes, num_experts)
    image_base = jnp.arange(local_images, dtype=jnp.int32)[:, None] * CAP
    position = (flat_routes * slot_count + image_base + slot_index).reshape(-1)
    token_ids = jnp.arange(local_images * 2 * tokens_dev, dtype=jnp.int32) // 2
    source = jnp.full((num_experts * slot_count,), -1, jnp.int32).at[position].set(token_ids)
    token_rows = normed_second.reshape(local_images * tokens_dev, width)
    gathered = jnp.take(token_rows, jnp.maximum(source, 0), axis=0)
    gathered = jnp.where(source[:, None] >= 0, gathered, jnp.zeros_like(gathered))
    outgoing = gathered.reshape(column_count, local_experts, slot_count, width)
    chunk_count = CHUNKS
    chunk = slot_count // chunk_count
    pieces = []
    for part in range(chunk_count):
        sent = outgoing[:, :, part * chunk:(part + 1) * chunk, :]
        by_column = lax.all_to_all(sent, "ep", split_axis=0, concat_axis=0, tiled=True)
        arrived = lax.all_gather(by_column, "node", axis=0, tiled=True)
        pre_act = jnp.einsum("lesd,edf->lesf", arrived, w_in, preferred_element_type=jnp.float32)
        hidden = jax.nn.gelu(pre_act, approximate=True).astype(jnp.bfloat16)
        partial_sum = jnp.einsum(
            "lesf,efd->lesd", hidden, w_out, preferred_element_type=jnp.float32
        ).astype(jnp.bfloat16)
        partial_sum = partial_sum.reshape(node_count * column_count * local_experts * chunk, width)
        summed = lax.psum_scatter(partial_sum, "node", scatter_dimension=0, tiled=True)
        summed = summed.reshape(column_count, local_experts, chunk, width)
        pieces.append(lax.all_to_all(summed, "ep", split_axis=0, concat_axis=0, tiled=True))
    expert_result = jnp.concatenate(pieces, axis=2)
    result_rows = expert_result.reshape(num_experts * slot_count, width)
    picked = jnp.take(result_rows, position, axis=0).reshape(local_images, tokens_dev, 2, width)
    expert_mix = jnp.sum(gate_values[..., None] * picked.astype(jnp.float32), axis=2)
    return (middle + expert_mix).astype(jnp.bfloat16)


def solution(mesh):
    placed = (
        P(("node", "ep"), None, None),
        P(None, "node"),
        P(None, "node"),
        P(None, "node"),
        P(),
        P(),
        P("ep", None, "node"),
        P("ep", "node", None),
        P(("node", "ep"), None, None),
    )
    return jax.shard_map(
        shards, mesh=mesh, in_specs=placed, out_specs=P(("node", "ep"), None, None), check_vma=False
    )
```

```python
import math

import jax
import jax.numpy as jnp
from jax import lax
from jax.sharding import PartitionSpec as P

D = 1280
HEADS = 16
CAP = 24


def layer_norm(values):
    center = values - jnp.mean(values, axis=-1, keepdims=True)
    spread = jnp.mean(center * center, axis=-1, keepdims=True)
    return center * lax.rsqrt(spread + 1e-06)


def slot_table(chosen, num_experts):
    onehot = (chosen[..., None] == jnp.arange(num_experts, dtype=jnp.int32)).astype(jnp.int32)
    before = jnp.cumsum(onehot, axis=1) - onehot
    return jnp.sum(before * onehot, axis=-1)


def shards(images, w_query, w_key, w_value, w_output, router, w_in, w_out, routes):
    local_images, tokens_dev, width = images.shape
    head_size = D // HEADS
    local_heads = w_query.shape[1] // head_size
    node_count = lax.axis_size("node")
    column_count = lax.axis_size("ep")
    num_experts = router.shape[1]
    local_experts = w_in.shape[0]
    slot_count = local_images * CAP
    inputs = images.astype(jnp.float32)
    normed = layer_norm(inputs).astype(jnp.bfloat16)
    shard_rows = lax.all_gather(normed, "node", axis=0, tiled=True)
    number = shard_rows.shape[0]
    queries = jnp.einsum(
        "ctd,de->cte", shard_rows, w_query, preferred_element_type=jnp.float32
    ).astype(jnp.bfloat16)
    projected_keys = jnp.einsum(
        "ctd,de->cte", shard_rows, w_key, preferred_element_type=jnp.float32
    ).astype(jnp.bfloat16)
    projected_values = jnp.einsum(
        "ctd,de->cte", shard_rows, w_value, preferred_element_type=jnp.float32
    ).astype(jnp.bfloat16)
    query_heads = queries.reshape(number, tokens_dev, local_heads, head_size)
    key_heads = projected_keys.reshape(number, tokens_dev, local_heads, head_size)
    value_heads = projected_values.reshape(number, tokens_dev, local_heads, head_size)
    scores = jnp.einsum(
        "cqhd,ckhd->chqk", query_heads, key_heads, preferred_element_type=jnp.float32
    ) / math.sqrt(head_size)
    weights = jax.nn.softmax(scores, axis=-1).astype(jnp.bfloat16)
    mixture = jnp.einsum(
        "chqk,ckhd->cqhd", weights, value_heads, preferred_element_type=jnp.float32
    ).astype(jnp.bfloat16)
    head_results = mixture.reshape(number, tokens_dev, local_heads * head_size)
    attention = jnp.einsum(
        "itd,de->ite",
        lax.all_to_all(head_results, "node", split_axis=0, concat_axis=2, tiled=True),
        w_output,
        preferred_element_type=jnp.float32,
    )
    middle = inputs + attention
    normed_second = layer_norm(middle).astype(jnp.bfloat16)
    logits = jnp.einsum("itd,de->ite", normed_second, router, preferred_element_type=jnp.float32)
    chosen_mask = routes[..., None] == jnp.arange(num_experts, dtype=jnp.int32)
    chosen_logit = jnp.sum(jnp.where(chosen_mask, logits[:, :, None, :], jnp.float32(0.0)), axis=-1)
    gate_values = jax.nn.sigmoid(chosen_logit)
    flat_routes = routes.reshape(local_images, 2 * tokens_dev)
    slot_index = slot_table(flat_routes, num_experts)
    image_base = jnp.arange(local_images, dtype=jnp.int32)[:, None] * CAP
    position = (flat_routes * slot_count + image_base + slot_index).reshape(-1)
    token_ids = jnp.arange(local_images * 2 * tokens_dev, dtype=jnp.int32) // 2
    source = jnp.full((num_experts * slot_count,), -1, jnp.int32).at[position].set(token_ids)
    token_rows = normed_second.reshape(local_images * tokens_dev, width)
    gathered = jnp.take(token_rows, jnp.maximum(source, 0), axis=0)
    gathered = jnp.where(source[:, None] >= 0, gathered, jnp.zeros_like(gathered))
    outgoing = gathered.reshape(column_count, local_experts, slot_count, width)
    copies = jnp.broadcast_to(outgoing[None], (node_count,) + outgoing.shape)
    copies = copies.reshape(node_count * column_count, local_experts, slot_count, width)
    arrived = lax.all_to_all(copies, ("node", "ep"), split_axis=0, concat_axis=0, tiled=True)
    rows = arrived.transpose(1, 0, 2, 3).reshape(local_experts, -1, width)
    pre_act = jnp.einsum("esd,edf->esf", rows, w_in, preferred_element_type=jnp.float32)
    hidden = jax.nn.gelu(pre_act, approximate=True).astype(jnp.bfloat16)
    partial_sum = jnp.einsum(
        "esf,efd->esd", hidden, w_out, preferred_element_type=jnp.float32
    ).astype(jnp.bfloat16)
    partial_sum = partial_sum.reshape(local_experts, node_count * column_count, slot_count, width)
    partial_sum = partial_sum.transpose(1, 0, 2, 3)
    returned = lax.all_to_all(partial_sum, ("node", "ep"), split_axis=0, concat_axis=0, tiled=True)
    returned = returned.astype(jnp.float32).reshape(
        node_count, column_count, local_experts, slot_count, width
    )
    expert_result = jnp.sum(returned, axis=0).astype(jnp.bfloat16)
    result_rows = expert_result.reshape(num_experts * slot_count, width)
    picked = jnp.take(result_rows, position, axis=0).reshape(local_images, tokens_dev, 2, width)
    expert_mix = jnp.sum(gate_values[..., None] * picked.astype(jnp.float32), axis=2)
    return (middle + expert_mix).astype(jnp.bfloat16)


def solution(mesh):
    placed = (
        P(("node", "ep"), None, None),
        P(None, "node"),
        P(None, "node"),
        P(None, "node"),
        P(),
        P(),
        P("ep", None, "node"),
        P("ep", "node", None),
        P(("node", "ep"), None, None),
    )
    return jax.shard_map(
        shards, mesh=mesh, in_specs=placed, out_specs=P(("node", "ep"), None, None), check_vma=False
    )
```

```python
import math

import jax
import jax.numpy as jnp
from jax import lax
from jax.sharding import PartitionSpec as P

D = 1280
HEADS = 16
CAP = 24


def layer_norm(values):
    center = values - jnp.mean(values, axis=-1, keepdims=True)
    spread = jnp.mean(center * center, axis=-1, keepdims=True)
    return center * lax.rsqrt(spread + 1e-06)


def slot_table(chosen, num_experts):
    onehot = (chosen[..., None] == jnp.arange(num_experts, dtype=jnp.int32)).astype(jnp.int32)
    before = jnp.cumsum(onehot, axis=1) - onehot
    return jnp.sum(before * onehot, axis=-1)


def shards(images, w_query, w_key, w_value, w_output, router, w_in, w_out, routes):
    local_images, tokens_dev, width = images.shape
    head_size = D // HEADS
    local_heads = w_query.shape[1] // head_size
    node_count = lax.axis_size("node")
    column_count = lax.axis_size("ep")
    num_experts = router.shape[1]
    local_experts = w_in.shape[0]
    slot_count = local_images * CAP
    inputs = images.astype(jnp.float32)
    normed = layer_norm(inputs).astype(jnp.bfloat16)
    shard_rows = lax.all_gather(normed, "node", axis=0, tiled=True)
    number = shard_rows.shape[0]
    queries = jnp.einsum(
        "ctd,de->cte", shard_rows, w_query, preferred_element_type=jnp.float32
    ).astype(jnp.bfloat16)
    projected_keys = jnp.einsum(
        "ctd,de->cte", shard_rows, w_key, preferred_element_type=jnp.float32
    ).astype(jnp.bfloat16)
    projected_values = jnp.einsum(
        "ctd,de->cte", shard_rows, w_value, preferred_element_type=jnp.float32
    ).astype(jnp.bfloat16)
    query_heads = queries.reshape(number, tokens_dev, local_heads, head_size)
    key_heads = projected_keys.reshape(number, tokens_dev, local_heads, head_size)
    value_heads = projected_values.reshape(number, tokens_dev, local_heads, head_size)
    scores = jnp.einsum(
        "cqhd,ckhd->chqk", query_heads, key_heads, preferred_element_type=jnp.float32
    ) / math.sqrt(head_size)
    weights = jax.nn.softmax(scores, axis=-1).astype(jnp.bfloat16)
    mixture = jnp.einsum(
        "chqk,ckhd->cqhd", weights, value_heads, preferred_element_type=jnp.float32
    ).astype(jnp.bfloat16)
    head_results = mixture.reshape(number, tokens_dev, local_heads * head_size)
    attention = jnp.einsum(
        "itd,de->ite",
        lax.all_to_all(head_results, "node", split_axis=0, concat_axis=2, tiled=True),
        w_output,
        preferred_element_type=jnp.float32,
    )
    middle = inputs + attention
    normed_second = layer_norm(middle).astype(jnp.bfloat16)
    logits = jnp.einsum("itd,de->ite", normed_second, router, preferred_element_type=jnp.float32)
    chosen_mask = routes[..., None] == jnp.arange(num_experts, dtype=jnp.int32)
    chosen_logit = jnp.sum(jnp.where(chosen_mask, logits[:, :, None, :], jnp.float32(0.0)), axis=-1)
    gate_values = jax.nn.sigmoid(chosen_logit)
    flat_routes = routes.reshape(local_images, 2 * tokens_dev)
    slot_index = slot_table(flat_routes, num_experts)
    image_base = jnp.arange(local_images, dtype=jnp.int32)[:, None] * CAP
    position = (flat_routes * slot_count + image_base + slot_index).reshape(-1)
    token_ids = jnp.arange(local_images * 2 * tokens_dev, dtype=jnp.int32) // 2
    source = jnp.full((num_experts * slot_count,), -1, jnp.int32).at[position].set(token_ids)
    token_rows = normed_second.reshape(local_images * tokens_dev, width)
    gathered = jnp.take(token_rows, jnp.maximum(source, 0), axis=0)
    gathered = jnp.where(source[:, None] >= 0, gathered, jnp.zeros_like(gathered))
    outgoing = gathered.reshape(column_count, local_experts, slot_count, width)
    by_column = lax.all_to_all(outgoing, "ep", split_axis=0, concat_axis=0, tiled=True)
    block = by_column.reshape(-1, width)
    half = block.shape[0] // 2
    ahead = [(i, (i + 1) % node_count) for i in range(node_count)]
    behind = [(i, (i - 1) % node_count) for i in range(node_count)]
    from_behind = lax.ppermute(block, "node", ahead)
    from_ahead = lax.ppermute(block, "node", behind)
    far_low = lax.ppermute(from_behind[:half], "node", ahead)
    far_high = lax.ppermute(from_ahead[half:], "node", behind)
    far = jnp.concatenate([far_low, far_high], axis=0)

    def expert(rows):
        pre_act = jnp.dot(rows, w_in[0], preferred_element_type=jnp.float32)
        hidden = jax.nn.gelu(pre_act, approximate=True).astype(jnp.bfloat16)
        return jnp.dot(hidden, w_out[0], preferred_element_type=jnp.float32).astype(jnp.bfloat16)

    own_part = expert(block)
    next_part = expert(from_ahead)
    prev_part = expert(from_behind)
    far_part = expert(far)
    got_low = lax.ppermute(far_part[:half], "node", ahead)
    got_high = lax.ppermute(far_part[half:], "node", behind)
    to_next = jnp.concatenate(
        [next_part[:half].astype(jnp.float32) + got_low.astype(jnp.float32), next_part[half:].astype(jnp.float32)],
        axis=0,
    )
    to_prev = jnp.concatenate(
        [prev_part[:half].astype(jnp.float32), prev_part[half:].astype(jnp.float32) + got_high.astype(jnp.float32)],
        axis=0,
    )
    back_behind = lax.ppermute(to_next.astype(jnp.bfloat16), "node", ahead)
    back_ahead = lax.ppermute(to_prev.astype(jnp.bfloat16), "node", behind)
    summed = (
        own_part.astype(jnp.float32)
        + back_behind.astype(jnp.float32)
        + back_ahead.astype(jnp.float32)
    ).astype(jnp.bfloat16)
    summed = summed.reshape(column_count, local_experts, slot_count, width)
    expert_result = lax.all_to_all(summed, "ep", split_axis=0, concat_axis=0, tiled=True)
    result_rows = expert_result.reshape(num_experts * slot_count, width)
    picked = jnp.take(result_rows, position, axis=0).reshape(local_images, tokens_dev, 2, width)
    expert_mix = jnp.sum(gate_values[..., None] * picked.astype(jnp.float32), axis=2)
    return (middle + expert_mix).astype(jnp.bfloat16)


def solution(mesh):
    placed = (
        P(("node", "ep"), None, None),
        P(None, "node"),
        P(None, "node"),
        P(None, "node"),
        P(),
        P(),
        P("ep", None, "node"),
        P("ep", "node", None),
        P(("node", "ep"), None, None),
    )
    return jax.shard_map(
        shards, mesh=mesh, in_specs=placed, out_specs=P(("node", "ep"), None, None), check_vma=False
    )
```

```python
import math

import jax
import jax.numpy as jnp
from jax import lax
from jax.sharding import PartitionSpec as P

D = 1280
HEADS = 16
CAP = 24


def layer_norm(values):
    center = values - jnp.mean(values, axis=-1, keepdims=True)
    spread = jnp.mean(center * center, axis=-1, keepdims=True)
    return center * lax.rsqrt(spread + 1e-06)


def slot_table(chosen, num_experts):
    onehot = (chosen[..., None] == jnp.arange(num_experts, dtype=jnp.int32)).astype(jnp.int32)
    before = jnp.cumsum(onehot, axis=1) - onehot
    return jnp.sum(before * onehot, axis=-1)


def shards(images, w_query, w_key, w_value, w_output, router, w_in, w_out, routes):
    local_images, tokens_dev, width = images.shape
    head_size = D // HEADS
    local_heads = w_query.shape[1] // head_size
    node_count = lax.axis_size("node")
    column_count = lax.axis_size("ep")
    num_experts = router.shape[1]
    local_experts = w_in.shape[0]
    slot_count = local_images * CAP
    inputs = images.astype(jnp.float32)
    normed = layer_norm(inputs).astype(jnp.bfloat16)
    shard_rows = lax.all_gather(normed, "node", axis=0, tiled=True)
    number = shard_rows.shape[0]
    queries = jnp.einsum(
        "ctd,de->cte", shard_rows, w_query, preferred_element_type=jnp.float32
    ).astype(jnp.bfloat16)
    projected_keys = jnp.einsum(
        "ctd,de->cte", shard_rows, w_key, preferred_element_type=jnp.float32
    ).astype(jnp.bfloat16)
    projected_values = jnp.einsum(
        "ctd,de->cte", shard_rows, w_value, preferred_element_type=jnp.float32
    ).astype(jnp.bfloat16)
    query_heads = queries.reshape(number, tokens_dev, local_heads, head_size)
    key_heads = projected_keys.reshape(number, tokens_dev, local_heads, head_size)
    value_heads = projected_values.reshape(number, tokens_dev, local_heads, head_size)
    scores = jnp.einsum(
        "cqhd,ckhd->chqk", query_heads, key_heads, preferred_element_type=jnp.float32
    ) / math.sqrt(head_size)
    weights = jax.nn.softmax(scores, axis=-1).astype(jnp.bfloat16)
    mixture = jnp.einsum(
        "chqk,ckhd->cqhd", weights, value_heads, preferred_element_type=jnp.float32
    ).astype(jnp.bfloat16)
    head_results = mixture.reshape(number, tokens_dev, local_heads * head_size)
    attention = jnp.einsum(
        "itd,de->ite",
        lax.all_to_all(head_results, "node", split_axis=0, concat_axis=2, tiled=True),
        w_output,
        preferred_element_type=jnp.float32,
    )
    middle = inputs + attention
    normed_second = layer_norm(middle).astype(jnp.bfloat16)
    logits = jnp.einsum("itd,de->ite", normed_second, router, preferred_element_type=jnp.float32)
    chosen_mask = routes[..., None] == jnp.arange(num_experts, dtype=jnp.int32)
    chosen_logit = jnp.sum(jnp.where(chosen_mask, logits[:, :, None, :], jnp.float32(0.0)), axis=-1)
    gate_values = jax.nn.sigmoid(chosen_logit)
    flat_routes = routes.reshape(local_images, 2 * tokens_dev)
    slot_index = slot_table(flat_routes, num_experts)
    image_base = jnp.arange(local_images, dtype=jnp.int32)[:, None] * CAP
    position = (flat_routes * slot_count + image_base + slot_index).reshape(-1)
    token_count = local_images * tokens_dev
    token_slots = position.reshape(token_count, 2)
    slot_ids = jnp.arange(num_experts * slot_count, dtype=jnp.int32)
    token_rows = normed_second.reshape(token_count, width)
    hits = (token_slots[None, :, 0] == slot_ids[:, None]) | (token_slots[None, :, 1] == slot_ids[:, None])
    gathered = jnp.dot(
        hits.astype(jnp.bfloat16), token_rows, preferred_element_type=jnp.float32
    ).astype(jnp.bfloat16)
    outgoing = gathered.reshape(column_count, local_experts, slot_count, width)
    copies = jnp.broadcast_to(outgoing[None], (node_count,) + outgoing.shape)
    copies = copies.reshape(node_count * column_count, local_experts, slot_count, width)
    arrived = lax.all_to_all(copies, ("node", "ep"), split_axis=0, concat_axis=0, tiled=True)
    rows = arrived.transpose(1, 0, 2, 3).reshape(local_experts, -1, width)
    pre_act = jnp.einsum("esd,edf->esf", rows, w_in, preferred_element_type=jnp.float32)
    hidden = jax.nn.gelu(pre_act, approximate=True).astype(jnp.bfloat16)
    partial_sum = jnp.einsum(
        "esf,efd->esd", hidden, w_out, preferred_element_type=jnp.float32
    ).astype(jnp.bfloat16)
    partial_sum = partial_sum.reshape(local_experts, node_count * column_count, slot_count, width)
    partial_sum = partial_sum.transpose(1, 0, 2, 3)
    returned = lax.all_to_all(partial_sum, ("node", "ep"), split_axis=0, concat_axis=0, tiled=True)
    returned = returned.astype(jnp.float32).reshape(
        node_count, column_count, local_experts, slot_count, width
    )
    expert_result = jnp.sum(returned, axis=0).astype(jnp.bfloat16)
    result_rows = expert_result.reshape(num_experts * slot_count, width)
    flat_gates = gate_values.reshape(token_count, 2)
    combine = jnp.where(token_slots[:, 0:1] == slot_ids[None, :], flat_gates[:, 0:1], jnp.float32(0.0)) + jnp.where(
        token_slots[:, 1:2] == slot_ids[None, :], flat_gates[:, 1:2], jnp.float32(0.0)
    )
    expert_mix = jnp.dot(
        combine, result_rows.astype(jnp.float32), precision=lax.Precision.HIGHEST,
        preferred_element_type=jnp.float32,
    ).reshape(local_images, tokens_dev, width)
    return (middle + expert_mix).astype(jnp.bfloat16)


def solution(mesh):
    placed = (
        P(("node", "ep"), None, None),
        P(None, "node"),
        P(None, "node"),
        P(None, "node"),
        P(),
        P(),
        P("ep", None, "node"),
        P("ep", "node", None),
        P(("node", "ep"), None, None),
    )
    return jax.shard_map(
        shards, mesh=mesh, in_specs=placed, out_specs=P(("node", "ep"), None, None), check_vma=False
    )
```

```python
import math

import jax
import jax.numpy as jnp
from jax import lax
from jax.sharding import PartitionSpec as P

D = 1280
HEADS = 16
CAP = 24


def layer_norm(values):
    center = values - jnp.mean(values, axis=-1, keepdims=True)
    spread = jnp.mean(center * center, axis=-1, keepdims=True)
    return center * lax.rsqrt(spread + 1e-06)


def slot_table(chosen, num_experts):
    onehot = (chosen[..., None] == jnp.arange(num_experts, dtype=jnp.int32)).astype(jnp.int32)
    before = jnp.cumsum(onehot, axis=1) - onehot
    return jnp.sum(before * onehot, axis=-1)


def shards(images, w_query, w_key, w_value, w_output, router, w_in, w_out, routes):
    local_images, tokens_dev, width = images.shape
    head_size = D // HEADS
    local_heads = w_query.shape[1] // head_size
    node_count = lax.axis_size("node")
    column_count = lax.axis_size("ep")
    num_experts = router.shape[1]
    local_experts = w_in.shape[0]
    slot_count = local_images * CAP
    inputs = images.astype(jnp.float32)
    normed = layer_norm(inputs).astype(jnp.bfloat16)
    shard_rows = lax.all_gather(normed, "node", axis=0, tiled=True)
    number = shard_rows.shape[0]
    queries = jnp.einsum(
        "ctd,de->cet", shard_rows, w_query, preferred_element_type=jnp.float32
    ).astype(jnp.bfloat16)
    projected_keys = jnp.einsum(
        "ctd,de->cet", shard_rows, w_key, preferred_element_type=jnp.float32
    ).astype(jnp.bfloat16)
    projected_values = jnp.einsum(
        "ctd,de->cet", shard_rows, w_value, preferred_element_type=jnp.float32
    ).astype(jnp.bfloat16)
    query_heads = queries.reshape(number, local_heads, head_size, tokens_dev)
    key_heads = projected_keys.reshape(number, local_heads, head_size, tokens_dev)
    value_heads = projected_values.reshape(number, local_heads, head_size, tokens_dev)
    scores = jnp.einsum(
        "chdq,chdk->chqk", query_heads, key_heads, preferred_element_type=jnp.float32
    ) / math.sqrt(head_size)
    weights = jax.nn.softmax(scores, axis=-1).astype(jnp.bfloat16)
    mixture = jnp.einsum(
        "chqk,chdk->cqhd", weights, value_heads, preferred_element_type=jnp.float32
    ).astype(jnp.bfloat16)
    head_results = mixture.reshape(number, tokens_dev, local_heads * head_size)
    exchanged = lax.all_to_all(head_results, "node", split_axis=0, concat_axis=0, tiled=True)
    attention = jnp.einsum(
        "gtd,gde->te",
        exchanged,
        w_output.reshape(node_count, local_heads * head_size, width),
        preferred_element_type=jnp.float32,
    ).reshape(local_images, tokens_dev, width)
    middle = inputs + attention
    normed_second = layer_norm(middle).astype(jnp.bfloat16)
    logits = jnp.einsum("itd,de->ite", normed_second, router, preferred_element_type=jnp.float32)
    chosen_mask = routes[..., None] == jnp.arange(num_experts, dtype=jnp.int32)
    chosen_logit = jnp.sum(jnp.where(chosen_mask, logits[:, :, None, :], jnp.float32(0.0)), axis=-1)
    gate_values = jax.nn.sigmoid(chosen_logit)
    flat_routes = routes.reshape(local_images, 2 * tokens_dev)
    slot_index = slot_table(flat_routes, num_experts)
    image_base = jnp.arange(local_images, dtype=jnp.int32)[:, None] * CAP
    position = (flat_routes * slot_count + image_base + slot_index).reshape(-1)
    token_count = local_images * tokens_dev
    token_slots = position.reshape(token_count, 2)
    slot_ids = jnp.arange(num_experts * slot_count, dtype=jnp.int32)
    token_rows = normed_second.reshape(token_count, width)
    hits = (token_slots[None, :, 0] == slot_ids[:, None]) | (token_slots[None, :, 1] == slot_ids[:, None])
    gathered = jnp.dot(
        hits.astype(jnp.bfloat16), token_rows, preferred_element_type=jnp.float32
    ).astype(jnp.bfloat16)
    outgoing = gathered.reshape(column_count, local_experts, slot_count, width)
    copies = jnp.broadcast_to(outgoing[None], (node_count,) + outgoing.shape)
    copies = copies.reshape(node_count * column_count, local_experts, slot_count, width)
    arrived = lax.all_to_all(copies, ("node", "ep"), split_axis=0, concat_axis=0, tiled=True)
    rows = arrived.transpose(1, 0, 2, 3).reshape(local_experts, -1, width)
    pre_act = jnp.einsum("esd,edf->esf", rows, w_in, preferred_element_type=jnp.float32)
    hidden = jax.nn.gelu(pre_act, approximate=True).astype(jnp.bfloat16)
    partial_sum = jnp.einsum(
        "esf,efd->esd", hidden, w_out, preferred_element_type=jnp.float32
    ).astype(jnp.bfloat16)
    partial_sum = partial_sum.reshape(local_experts, node_count * column_count, slot_count, width)
    partial_sum = partial_sum.transpose(1, 0, 2, 3)
    returned = lax.all_to_all(partial_sum, ("node", "ep"), split_axis=0, concat_axis=0, tiled=True)
    returned = returned.astype(jnp.float32).reshape(
        node_count, column_count, local_experts, slot_count, width
    )
    expert_result = jnp.sum(returned, axis=0).astype(jnp.bfloat16)
    result_rows = expert_result.reshape(num_experts * slot_count, width)
    flat_gates = gate_values.reshape(token_count, 2)
    combine = jnp.where(token_slots[:, 0:1] == slot_ids[None, :], flat_gates[:, 0:1], jnp.float32(0.0)) + jnp.where(
        token_slots[:, 1:2] == slot_ids[None, :], flat_gates[:, 1:2], jnp.float32(0.0)
    )
    expert_mix = jnp.dot(
        combine, result_rows.astype(jnp.float32), precision=lax.Precision.HIGHEST,
        preferred_element_type=jnp.float32,
    ).reshape(local_images, tokens_dev, width)
    return (middle + expert_mix).astype(jnp.bfloat16)


def solution(mesh):
    placed = (
        P(("node", "ep"), None, None),
        P(None, "node"),
        P(None, "node"),
        P(None, "node"),
        P(),
        P(),
        P("ep", None, "node"),
        P("ep", "node", None),
        P(("node", "ep"), None, None),
    )
    return jax.shard_map(
        shards, mesh=mesh, in_specs=placed, out_specs=P(("node", "ep"), None, None), check_vma=False
    )
```

```python
import math

import jax
import jax.numpy as jnp
from jax import lax
from jax.sharding import PartitionSpec as P

D = 1280
HEADS = 16
CAP = 24


def layer_norm(values):
    center = values - jnp.mean(values, axis=-1, keepdims=True)
    spread = jnp.mean(center * center, axis=-1, keepdims=True)
    return center * lax.rsqrt(spread + 1e-06)


def slot_table(chosen, num_experts):
    onehot = (chosen[..., None] == jnp.arange(num_experts, dtype=jnp.int32)).astype(jnp.int32)
    before = jnp.cumsum(onehot, axis=1) - onehot
    return jnp.sum(before * onehot, axis=-1)


def shards(images, w_query, w_key, w_value, w_output, router, w_in, w_out, routes):
    local_images, tokens_dev, width = images.shape
    head_size = D // HEADS
    local_heads = w_query.shape[1] // head_size
    node_count = lax.axis_size("node")
    column_count = lax.axis_size("ep")
    num_experts = router.shape[1]
    local_experts = w_in.shape[0]
    slot_count = local_images * CAP
    inputs = images.astype(jnp.float32)
    normed = layer_norm(inputs).astype(jnp.bfloat16)
    node_index = lax.axis_index("node")
    ahead = [(i, (i + 1) % node_count) for i in range(node_count)]
    behind = [(i, (i - 1) % node_count) for i in range(node_count)]
    split = width // 2
    from_behind = lax.ppermute(normed, "node", ahead)
    from_ahead = lax.ppermute(normed, "node", behind)
    far = jnp.concatenate(
        [
            lax.ppermute(from_behind[..., :split], "node", ahead),
            lax.ppermute(from_ahead[..., split:], "node", behind),
        ],
        axis=-1,
    )
    shard_rows = jnp.concatenate([normed, from_ahead, far, from_behind], axis=0)
    number = shard_rows.shape[0]
    queries = jnp.einsum(
        "ctd,de->cet", shard_rows, w_query, preferred_element_type=jnp.float32
    ).astype(jnp.bfloat16)
    projected_keys = jnp.einsum(
        "ctd,de->cet", shard_rows, w_key, preferred_element_type=jnp.float32
    ).astype(jnp.bfloat16)
    projected_values = jnp.einsum(
        "ctd,de->cet", shard_rows, w_value, preferred_element_type=jnp.float32
    ).astype(jnp.bfloat16)
    query_heads = queries.reshape(number, local_heads, head_size, tokens_dev)
    key_heads = projected_keys.reshape(number, local_heads, head_size, tokens_dev)
    value_heads = projected_values.reshape(number, local_heads, head_size, tokens_dev)
    scores = jnp.einsum(
        "chdq,chdk->chqk", query_heads, key_heads, preferred_element_type=jnp.float32
    ) / math.sqrt(head_size)
    weights = jax.nn.softmax(scores, axis=-1).astype(jnp.bfloat16)
    mixture = jnp.einsum(
        "chqk,chdk->cqhd", weights, value_heads, preferred_element_type=jnp.float32
    ).astype(jnp.bfloat16)
    head_results = jnp.roll(mixture.reshape(number, tokens_dev, local_heads * head_size), node_index, axis=0)
    exchanged = lax.all_to_all(head_results, "node", split_axis=0, concat_axis=0, tiled=True)
    attention = jnp.einsum(
        "gtd,gde->te",
        exchanged,
        w_output.reshape(node_count, local_heads * head_size, width),
        preferred_element_type=jnp.float32,
    ).reshape(local_images, tokens_dev, width)
    middle = inputs + attention
    normed_second = layer_norm(middle).astype(jnp.bfloat16)
    logits = jnp.einsum("itd,de->ite", normed_second, router, preferred_element_type=jnp.float32)
    chosen_mask = routes[..., None] == jnp.arange(num_experts, dtype=jnp.int32)
    chosen_logit = jnp.sum(jnp.where(chosen_mask, logits[:, :, None, :], jnp.float32(0.0)), axis=-1)
    gate_values = jax.nn.sigmoid(chosen_logit)
    flat_routes = routes.reshape(local_images, 2 * tokens_dev)
    slot_index = slot_table(flat_routes, num_experts)
    image_base = jnp.arange(local_images, dtype=jnp.int32)[:, None] * CAP
    position = (flat_routes * slot_count + image_base + slot_index).reshape(-1)
    token_count = local_images * tokens_dev
    token_slots = position.reshape(token_count, 2)
    slot_ids = jnp.arange(num_experts * slot_count, dtype=jnp.int32)
    token_rows = normed_second.reshape(token_count, width)
    hits = (token_slots[None, :, 0] == slot_ids[:, None]) | (token_slots[None, :, 1] == slot_ids[:, None])
    gathered = jnp.dot(
        hits.astype(jnp.bfloat16), token_rows, preferred_element_type=jnp.float32
    ).astype(jnp.bfloat16)
    outgoing = gathered.reshape(column_count, local_experts, slot_count, width)
    copies = jnp.broadcast_to(outgoing[None], (node_count,) + outgoing.shape)
    copies = copies.reshape(node_count * column_count, local_experts, slot_count, width)
    arrived = lax.all_to_all(copies, ("node", "ep"), split_axis=0, concat_axis=0, tiled=True)
    rows = arrived.transpose(1, 0, 2, 3).reshape(local_experts, -1, width)
    pre_act = jnp.einsum("esd,edf->esf", rows, w_in, preferred_element_type=jnp.float32)
    hidden = jax.nn.gelu(pre_act, approximate=True).astype(jnp.bfloat16)
    partial_sum = jnp.einsum(
        "esf,efd->esd", hidden, w_out, preferred_element_type=jnp.float32
    ).astype(jnp.bfloat16)
    partial_sum = partial_sum.reshape(local_experts, node_count * column_count, slot_count, width)
    partial_sum = partial_sum.transpose(1, 0, 2, 3)
    returned = lax.all_to_all(partial_sum, ("node", "ep"), split_axis=0, concat_axis=0, tiled=True)
    returned = returned.astype(jnp.float32).reshape(
        node_count, column_count, local_experts, slot_count, width
    )
    expert_result = jnp.sum(returned, axis=0).astype(jnp.bfloat16)
    result_rows = expert_result.reshape(num_experts * slot_count, width)
    flat_gates = gate_values.reshape(token_count, 2)
    combine = jnp.where(token_slots[:, 0:1] == slot_ids[None, :], flat_gates[:, 0:1], jnp.float32(0.0)) + jnp.where(
        token_slots[:, 1:2] == slot_ids[None, :], flat_gates[:, 1:2], jnp.float32(0.0)
    )
    expert_mix = jnp.dot(
        combine, result_rows.astype(jnp.float32), precision=lax.Precision.HIGHEST,
        preferred_element_type=jnp.float32,
    ).reshape(local_images, tokens_dev, width)
    return (middle + expert_mix).astype(jnp.bfloat16)


def solution(mesh):
    placed = (
        P(("node", "ep"), None, None),
        P(None, "node"),
        P(None, "node"),
        P(None, "node"),
        P(),
        P(),
        P("ep", None, "node"),
        P("ep", "node", None),
        P(("node", "ep"), None, None),
    )
    return jax.shard_map(
        shards, mesh=mesh, in_specs=placed, out_specs=P(("node", "ep"), None, None), check_vma=False
    )
```

```python
import math

import jax
import jax.numpy as jnp
from jax import lax
from jax.sharding import PartitionSpec as P

D = 1280
HEADS = 16
CAP = 24
MOE_CHUNKS = 2


def layer_norm(values):
    center = values - jnp.mean(values, axis=-1, keepdims=True)
    spread = jnp.mean(center * center, axis=-1, keepdims=True)
    return center * lax.rsqrt(spread + 1e-06)


def slot_table(chosen, num_experts):
    onehot = (chosen[..., None] == jnp.arange(num_experts, dtype=jnp.int32)).astype(jnp.int32)
    before = jnp.cumsum(onehot, axis=1) - onehot
    return jnp.sum(before * onehot, axis=-1)


def shards(images, w_query, w_key, w_value, w_output, router, w_in, w_out, routes):
    local_images, tokens_dev, width = images.shape
    head_size = D // HEADS
    local_heads = w_query.shape[1] // head_size
    node_count = lax.axis_size("node")
    column_count = lax.axis_size("ep")
    num_experts = router.shape[1]
    local_experts = w_in.shape[0]
    slot_count = local_images * CAP
    inputs = images.astype(jnp.float32)
    normed = layer_norm(inputs).astype(jnp.bfloat16)
    node_index = lax.axis_index("node")
    ahead = [(i, (i + 1) % node_count) for i in range(node_count)]
    behind = [(i, (i - 1) % node_count) for i in range(node_count)]
    split = width // 2
    from_behind = lax.ppermute(normed, "node", ahead)
    from_ahead = lax.ppermute(normed, "node", behind)
    far = jnp.concatenate(
        [
            lax.ppermute(from_behind[..., :split], "node", ahead),
            lax.ppermute(from_ahead[..., split:], "node", behind),
        ],
        axis=-1,
    )
    shard_rows = jnp.concatenate([normed, from_ahead, far, from_behind], axis=0)
    number = shard_rows.shape[0]
    queries = jnp.einsum(
        "ctd,de->cet", shard_rows, w_query, preferred_element_type=jnp.float32
    ).astype(jnp.bfloat16)
    projected_keys = jnp.einsum(
        "ctd,de->cet", shard_rows, w_key, preferred_element_type=jnp.float32
    ).astype(jnp.bfloat16)
    projected_values = jnp.einsum(
        "ctd,de->cet", shard_rows, w_value, preferred_element_type=jnp.float32
    ).astype(jnp.bfloat16)
    query_heads = queries.reshape(number, local_heads, head_size, tokens_dev)
    key_heads = projected_keys.reshape(number, local_heads, head_size, tokens_dev)
    value_heads = projected_values.reshape(number, local_heads, head_size, tokens_dev)
    scores = jnp.einsum(
        "chdq,chdk->chqk", query_heads, key_heads, preferred_element_type=jnp.float32
    ) / math.sqrt(head_size)
    weights = jax.nn.softmax(scores, axis=-1).astype(jnp.bfloat16)
    mixture = jnp.einsum(
        "chqk,chdk->cqhd", weights, value_heads, preferred_element_type=jnp.float32
    ).astype(jnp.bfloat16)
    head_results = jnp.roll(mixture.reshape(number, tokens_dev, local_heads * head_size), node_index, axis=0)
    exchanged = lax.all_to_all(head_results, "node", split_axis=0, concat_axis=0, tiled=True)
    attention = jnp.einsum(
        "gtd,gde->te",
        exchanged,
        w_output.reshape(node_count, local_heads * head_size, width),
        preferred_element_type=jnp.float32,
    ).reshape(local_images, tokens_dev, width)
    middle = inputs + attention
    normed_second = layer_norm(middle).astype(jnp.bfloat16)
    logits = jnp.einsum("itd,de->ite", normed_second, router, preferred_element_type=jnp.float32)
    chosen_mask = routes[..., None] == jnp.arange(num_experts, dtype=jnp.int32)
    chosen_logit = jnp.sum(jnp.where(chosen_mask, logits[:, :, None, :], jnp.float32(0.0)), axis=-1)
    gate_values = jax.nn.sigmoid(chosen_logit)
    flat_routes = routes.reshape(local_images, 2 * tokens_dev)
    slot_index = slot_table(flat_routes, num_experts)
    image_base = jnp.arange(local_images, dtype=jnp.int32)[:, None] * CAP
    position = (flat_routes * slot_count + image_base + slot_index).reshape(-1)
    token_count = local_images * tokens_dev
    token_slots = position.reshape(token_count, 2)
    slot_ids = jnp.arange(num_experts * slot_count, dtype=jnp.int32)
    token_rows = normed_second.reshape(token_count, width)
    hits = (token_slots[None, :, 0] == slot_ids[:, None]) | (token_slots[None, :, 1] == slot_ids[:, None])
    gathered = jnp.dot(
        hits.astype(jnp.bfloat16), token_rows, preferred_element_type=jnp.float32
    ).astype(jnp.bfloat16)
    outgoing = gathered.reshape(column_count, local_experts, slot_count, width)
    chunk = slot_count // MOE_CHUNKS
    pieces = []
    for part in range(MOE_CHUNKS):
        sent = outgoing[:, :, part * chunk:(part + 1) * chunk, :]
        block = lax.all_to_all(sent, "ep", split_axis=0, concat_axis=0, tiled=True).reshape(-1, width)
        half = block.shape[0] // 2
        came_behind = lax.ppermute(block, "node", ahead)
        came_ahead = lax.ppermute(block, "node", behind)
        came_far = jnp.concatenate(
            [
                lax.ppermute(came_behind[:half], "node", ahead),
                lax.ppermute(came_ahead[half:], "node", behind),
            ],
            axis=0,
        )
        rows = jnp.concatenate([block, came_ahead, came_far, came_behind], axis=0)
        pre_act = jnp.dot(rows, w_in[0], preferred_element_type=jnp.float32)
        hidden = jax.nn.gelu(pre_act, approximate=True).astype(jnp.bfloat16)
        partial_sum = jnp.dot(hidden, w_out[0], preferred_element_type=jnp.float32).astype(jnp.bfloat16)
        own_part, next_part, far_part, prev_part = jnp.split(partial_sum, node_count, axis=0)
        got_low = lax.ppermute(far_part[:half], "node", ahead).astype(jnp.float32)
        got_high = lax.ppermute(far_part[half:], "node", behind).astype(jnp.float32)
        to_next = jnp.concatenate(
            [next_part[:half].astype(jnp.float32) + got_low, next_part[half:].astype(jnp.float32)], axis=0
        )
        to_prev = jnp.concatenate(
            [prev_part[:half].astype(jnp.float32), prev_part[half:].astype(jnp.float32) + got_high], axis=0
        )
        back_behind = lax.ppermute(to_next.astype(jnp.bfloat16), "node", ahead)
        back_ahead = lax.ppermute(to_prev.astype(jnp.bfloat16), "node", behind)
        summed = (
            own_part.astype(jnp.float32) + back_behind.astype(jnp.float32) + back_ahead.astype(jnp.float32)
        ).astype(jnp.bfloat16)
        summed = summed.reshape(column_count, local_experts, chunk, width)
        pieces.append(lax.all_to_all(summed, "ep", split_axis=0, concat_axis=0, tiled=True))
    expert_result = jnp.concatenate(pieces, axis=2)
    result_rows = expert_result.reshape(num_experts * slot_count, width)
    flat_gates = gate_values.reshape(token_count, 2)
    combine = jnp.where(token_slots[:, 0:1] == slot_ids[None, :], flat_gates[:, 0:1], jnp.float32(0.0)) + jnp.where(
        token_slots[:, 1:2] == slot_ids[None, :], flat_gates[:, 1:2], jnp.float32(0.0)
    )
    expert_mix = jnp.dot(
        combine, result_rows.astype(jnp.float32), precision=lax.Precision.HIGHEST,
        preferred_element_type=jnp.float32,
    ).reshape(local_images, tokens_dev, width)
    return (middle + expert_mix).astype(jnp.bfloat16)


def solution(mesh):
    placed = (
        P(("node", "ep"), None, None),
        P(None, "node"),
        P(None, "node"),
        P(None, "node"),
        P(),
        P(),
        P("ep", None, "node"),
        P("ep", "node", None),
        P(("node", "ep"), None, None),
    )
    return jax.shard_map(
        shards, mesh=mesh, in_specs=placed, out_specs=P(("node", "ep"), None, None), check_vma=False
    )
```

```python
import math

import jax
import jax.numpy as jnp
from jax import lax
from jax.sharding import PartitionSpec as P

D = 1280
HEADS = 16
CAP = 24
MOE_CHUNKS = 3


def layer_norm(values):
    center = values - jnp.mean(values, axis=-1, keepdims=True)
    spread = jnp.mean(center * center, axis=-1, keepdims=True)
    return center * lax.rsqrt(spread + 1e-06)


def slot_table(chosen, num_experts):
    onehot = (chosen[..., None] == jnp.arange(num_experts, dtype=jnp.int32)).astype(jnp.int32)
    before = jnp.cumsum(onehot, axis=1) - onehot
    return jnp.sum(before * onehot, axis=-1)


def shards(images, w_query, w_key, w_value, w_output, router, w_in, w_out, routes):
    local_images, tokens_dev, width = images.shape
    head_size = D // HEADS
    local_heads = w_query.shape[1] // head_size
    node_count = lax.axis_size("node")
    column_count = lax.axis_size("ep")
    num_experts = router.shape[1]
    local_experts = w_in.shape[0]
    slot_count = local_images * CAP
    inputs = images.astype(jnp.float32)
    normed = layer_norm(inputs).astype(jnp.bfloat16)
    node_index = lax.axis_index("node")
    ahead = [(i, (i + 1) % node_count) for i in range(node_count)]
    behind = [(i, (i - 1) % node_count) for i in range(node_count)]
    split = width // 2
    from_behind = lax.ppermute(normed, "node", ahead)
    from_ahead = lax.ppermute(normed, "node", behind)
    far = jnp.concatenate(
        [
            lax.ppermute(from_behind[..., :split], "node", ahead),
            lax.ppermute(from_ahead[..., split:], "node", behind),
        ],
        axis=-1,
    )
    shard_rows = jnp.concatenate([normed, from_ahead, far, from_behind], axis=0)
    number = shard_rows.shape[0]
    queries = jnp.einsum(
        "ctd,de->cet", shard_rows, w_query, preferred_element_type=jnp.float32
    ).astype(jnp.bfloat16)
    projected_keys = jnp.einsum(
        "ctd,de->cet", shard_rows, w_key, preferred_element_type=jnp.float32
    ).astype(jnp.bfloat16)
    projected_values = jnp.einsum(
        "ctd,de->cet", shard_rows, w_value, preferred_element_type=jnp.float32
    ).astype(jnp.bfloat16)
    query_heads = queries.reshape(number, local_heads, head_size, tokens_dev)
    key_heads = projected_keys.reshape(number, local_heads, head_size, tokens_dev)
    value_heads = projected_values.reshape(number, local_heads, head_size, tokens_dev)
    scores = jnp.einsum(
        "chdq,chdk->chqk", query_heads, key_heads, preferred_element_type=jnp.float32
    ) / math.sqrt(head_size)
    weights = jax.nn.softmax(scores, axis=-1).astype(jnp.bfloat16)
    mixture = jnp.einsum(
        "chqk,chdk->cqhd", weights, value_heads, preferred_element_type=jnp.float32
    ).astype(jnp.bfloat16)
    head_results = jnp.roll(mixture.reshape(number, tokens_dev, local_heads * head_size), node_index, axis=0)
    exchanged = lax.all_to_all(head_results, "node", split_axis=0, concat_axis=0, tiled=True)
    attention = jnp.einsum(
        "gtd,gde->te",
        exchanged,
        w_output.reshape(node_count, local_heads * head_size, width),
        preferred_element_type=jnp.float32,
    ).reshape(local_images, tokens_dev, width)
    middle = inputs + attention
    normed_second = layer_norm(middle).astype(jnp.bfloat16)
    logits = jnp.einsum("itd,de->ite", normed_second, router, preferred_element_type=jnp.float32)
    chosen_mask = routes[..., None] == jnp.arange(num_experts, dtype=jnp.int32)
    chosen_logit = jnp.sum(jnp.where(chosen_mask, logits[:, :, None, :], jnp.float32(0.0)), axis=-1)
    gate_values = jax.nn.sigmoid(chosen_logit)
    flat_routes = routes.reshape(local_images, 2 * tokens_dev)
    slot_index = slot_table(flat_routes, num_experts)
    image_base = jnp.arange(local_images, dtype=jnp.int32)[:, None] * CAP
    position = (flat_routes * slot_count + image_base + slot_index).reshape(-1)
    token_count = local_images * tokens_dev
    token_slots = position.reshape(token_count, 2)
    slot_ids = jnp.arange(num_experts * slot_count, dtype=jnp.int32)
    token_rows = normed_second.reshape(token_count, width)
    hits = (token_slots[None, :, 0] == slot_ids[:, None]) | (token_slots[None, :, 1] == slot_ids[:, None])
    gathered = jnp.dot(
        hits.astype(jnp.bfloat16), token_rows, preferred_element_type=jnp.float32
    ).astype(jnp.bfloat16)
    outgoing = gathered.reshape(column_count, local_experts, slot_count, width)
    chunk = slot_count // MOE_CHUNKS
    pieces = []
    for part in range(MOE_CHUNKS):
        sent = outgoing[:, :, part * chunk:(part + 1) * chunk, :]
        block = lax.all_to_all(sent, "ep", split_axis=0, concat_axis=0, tiled=True).reshape(-1, width)
        half = block.shape[0] // 2
        came_behind = lax.ppermute(block, "node", ahead)
        came_ahead = lax.ppermute(block, "node", behind)
        came_far = jnp.concatenate(
            [
                lax.ppermute(came_behind[:half], "node", ahead),
                lax.ppermute(came_ahead[half:], "node", behind),
            ],
            axis=0,
        )
        rows = jnp.concatenate([block, came_ahead, came_far, came_behind], axis=0)
        pre_act = jnp.dot(rows, w_in[0], preferred_element_type=jnp.float32)
        hidden = jax.nn.gelu(pre_act, approximate=True).astype(jnp.bfloat16)
        partial_sum = jnp.dot(hidden, w_out[0], preferred_element_type=jnp.float32).astype(jnp.bfloat16)
        own_part, next_part, far_part, prev_part = jnp.split(partial_sum, node_count, axis=0)
        got_low = lax.ppermute(far_part[:half], "node", ahead).astype(jnp.float32)
        got_high = lax.ppermute(far_part[half:], "node", behind).astype(jnp.float32)
        to_next = jnp.concatenate(
            [next_part[:half].astype(jnp.float32) + got_low, next_part[half:].astype(jnp.float32)], axis=0
        )
        to_prev = jnp.concatenate(
            [prev_part[:half].astype(jnp.float32), prev_part[half:].astype(jnp.float32) + got_high], axis=0
        )
        back_behind = lax.ppermute(to_next.astype(jnp.bfloat16), "node", ahead)
        back_ahead = lax.ppermute(to_prev.astype(jnp.bfloat16), "node", behind)
        summed = (
            own_part.astype(jnp.float32) + back_behind.astype(jnp.float32) + back_ahead.astype(jnp.float32)
        ).astype(jnp.bfloat16)
        summed = summed.reshape(column_count, local_experts, chunk, width)
        pieces.append(lax.all_to_all(summed, "ep", split_axis=0, concat_axis=0, tiled=True))
    expert_result = jnp.concatenate(pieces, axis=2)
    result_rows = expert_result.reshape(num_experts * slot_count, width)
    flat_gates = gate_values.reshape(token_count, 2)
    combine = jnp.where(token_slots[:, 0:1] == slot_ids[None, :], flat_gates[:, 0:1], jnp.float32(0.0)) + jnp.where(
        token_slots[:, 1:2] == slot_ids[None, :], flat_gates[:, 1:2], jnp.float32(0.0)
    )
    expert_mix = jnp.dot(
        combine, result_rows.astype(jnp.float32), precision=lax.Precision.HIGHEST,
        preferred_element_type=jnp.float32,
    ).reshape(local_images, tokens_dev, width)
    return (middle + expert_mix).astype(jnp.bfloat16)


def solution(mesh):
    placed = (
        P(("node", "ep"), None, None),
        P(None, "node"),
        P(None, "node"),
        P(None, "node"),
        P(),
        P(),
        P("ep", None, "node"),
        P("ep", "node", None),
        P(("node", "ep"), None, None),
    )
    return jax.shard_map(
        shards, mesh=mesh, in_specs=placed, out_specs=P(("node", "ep"), None, None), check_vma=False
    )
```

```python
import math

import jax
import jax.numpy as jnp
from jax import lax
from jax.sharding import PartitionSpec as P

D = 1280
HEADS = 16
CAP = 24
MOE_CHUNKS = 2


def layer_norm(values):
    center = values - jnp.mean(values, axis=-1, keepdims=True)
    spread = jnp.mean(center * center, axis=-1, keepdims=True)
    return center * lax.rsqrt(spread + 1e-06)


def slot_table(chosen, num_experts):
    onehot = (chosen[..., None] == jnp.arange(num_experts, dtype=jnp.int32)).astype(jnp.int32)
    before = jnp.cumsum(onehot, axis=1) - onehot
    return jnp.sum(before * onehot, axis=-1)


def shards(images, w_query, w_key, w_value, w_output, router, w_in, w_out, routes):
    local_images, tokens_dev, width = images.shape
    head_size = D // HEADS
    local_heads = w_query.shape[1] // head_size
    node_count = lax.axis_size("node")
    column_count = lax.axis_size("ep")
    num_experts = router.shape[1]
    local_experts = w_in.shape[0]
    slot_count = local_images * CAP
    inputs = images.astype(jnp.float32)
    normed = layer_norm(inputs).astype(jnp.bfloat16)
    node_index = lax.axis_index("node")
    ahead = [(i, (i + 1) % node_count) for i in range(node_count)]
    behind = [(i, (i - 1) % node_count) for i in range(node_count)]
    split = width // 2
    from_behind = lax.ppermute(normed, "node", ahead)
    from_ahead = lax.ppermute(normed, "node", behind)
    far = jnp.concatenate(
        [
            lax.ppermute(from_behind[..., :split], "node", ahead),
            lax.ppermute(from_ahead[..., split:], "node", behind),
        ],
        axis=-1,
    )
    shard_rows = jnp.concatenate([normed, from_ahead, far, from_behind], axis=0)
    number = shard_rows.shape[0]
    queries = jnp.einsum(
        "ctd,de->cet", shard_rows, w_query, preferred_element_type=jnp.float32
    ).astype(jnp.bfloat16)
    projected_keys = jnp.einsum(
        "ctd,de->cet", shard_rows, w_key, preferred_element_type=jnp.float32
    ).astype(jnp.bfloat16)
    projected_values = jnp.einsum(
        "ctd,de->cet", shard_rows, w_value, preferred_element_type=jnp.float32
    ).astype(jnp.bfloat16)
    query_heads = queries.reshape(number, local_heads, head_size, tokens_dev)
    key_heads = projected_keys.reshape(number, local_heads, head_size, tokens_dev)
    value_heads = projected_values.reshape(number, local_heads, head_size, tokens_dev)
    scores = jnp.einsum(
        "chdq,chdk->chqk", query_heads, key_heads, preferred_element_type=jnp.float32
    ) / math.sqrt(head_size)
    weights = jax.nn.softmax(scores, axis=-1).astype(jnp.bfloat16)
    mixture = jnp.einsum(
        "chqk,chdk->cqhd", weights, value_heads, preferred_element_type=jnp.float32
    ).astype(jnp.bfloat16)
    head_results = jnp.roll(mixture.reshape(number, tokens_dev, local_heads * head_size), node_index, axis=0)
    exchanged = lax.all_to_all(head_results, "node", split_axis=0, concat_axis=0, tiled=True)
    attention = jnp.einsum(
        "gtd,gde->te",
        exchanged,
        w_output.reshape(node_count, local_heads * head_size, width),
        preferred_element_type=jnp.float32,
    ).reshape(local_images, tokens_dev, width)
    middle = inputs + attention
    normed_second = layer_norm(middle).astype(jnp.bfloat16)
    logits = jnp.einsum("itd,de->ite", normed_second, router, preferred_element_type=jnp.float32)
    chosen_mask = routes[..., None] == jnp.arange(num_experts, dtype=jnp.int32)
    chosen_logit = jnp.sum(jnp.where(chosen_mask, logits[:, :, None, :], jnp.float32(0.0)), axis=-1)
    gate_values = jax.nn.sigmoid(chosen_logit)
    flat_routes = routes.reshape(local_images, 2 * tokens_dev)
    slot_index = slot_table(flat_routes, num_experts)
    image_base = jnp.arange(local_images, dtype=jnp.int32)[:, None] * CAP
    position = (flat_routes * slot_count + image_base + slot_index).reshape(-1)
    token_count = local_images * tokens_dev
    token_slots = position.reshape(token_count, 2)
    slot_ids = jnp.arange(num_experts * slot_count, dtype=jnp.int32)
    token_rows = normed_second.reshape(token_count, width)
    hits = (token_slots[None, :, 0] == slot_ids[:, None]) | (token_slots[None, :, 1] == slot_ids[:, None])
    gathered = jnp.dot(
        hits.astype(jnp.bfloat16), token_rows, preferred_element_type=jnp.float32
    ).astype(jnp.bfloat16)
    outgoing = gathered.reshape(column_count, local_experts, slot_count, width)
    chunk = slot_count // MOE_CHUNKS
    pieces = []
    pending = None
    for part in range(MOE_CHUNKS):
        sent = outgoing[:, :, part * chunk:(part + 1) * chunk, :]
        block = lax.all_to_all(sent, "ep", split_axis=0, concat_axis=0, tiled=True).reshape(-1, width)
        half = block.shape[0] // 2
        came_behind = lax.ppermute(block, "node", ahead)
        came_ahead = lax.ppermute(block, "node", behind)
        came_far = jnp.concatenate(
            [
                lax.ppermute(came_behind[:half], "node", ahead),
                lax.ppermute(came_ahead[half:], "node", behind),
            ],
            axis=0,
        )
        rows = jnp.concatenate([block, came_ahead, came_far, came_behind], axis=0)
        pre_act = jnp.dot(rows, w_in[0], preferred_element_type=jnp.float32)
        hidden = jax.nn.gelu(pre_act, approximate=True).astype(jnp.bfloat16)
        partial_sum = jnp.dot(hidden, w_out[0], preferred_element_type=jnp.float32).astype(jnp.bfloat16)
        own_part, next_part, far_part, prev_part = jnp.split(partial_sum, node_count, axis=0)
        got_low = lax.ppermute(far_part[:half], "node", ahead).astype(jnp.float32)
        got_high = lax.ppermute(far_part[half:], "node", behind).astype(jnp.float32)
        to_next = jnp.concatenate(
            [next_part[:half].astype(jnp.float32) + got_low, next_part[half:].astype(jnp.float32)], axis=0
        )
        to_prev = jnp.concatenate(
            [prev_part[:half].astype(jnp.float32), prev_part[half:].astype(jnp.float32) + got_high], axis=0
        )
        if pending is not None:
            pending, to_next, to_prev = lax.optimization_barrier((pending, to_next, to_prev))
            pieces.append(lax.all_to_all(pending, "ep", split_axis=0, concat_axis=0, tiled=True))
        back_behind = lax.ppermute(to_next.astype(jnp.bfloat16), "node", ahead)
        back_ahead = lax.ppermute(to_prev.astype(jnp.bfloat16), "node", behind)
        summed = (
            own_part.astype(jnp.float32) + back_behind.astype(jnp.float32) + back_ahead.astype(jnp.float32)
        ).astype(jnp.bfloat16)
        pending = summed.reshape(column_count, local_experts, chunk, width)
    pieces.append(lax.all_to_all(pending, "ep", split_axis=0, concat_axis=0, tiled=True))
    expert_result = jnp.concatenate(pieces, axis=2)
    result_rows = expert_result.reshape(num_experts * slot_count, width)
    flat_gates = gate_values.reshape(token_count, 2)
    combine = jnp.where(token_slots[:, 0:1] == slot_ids[None, :], flat_gates[:, 0:1], jnp.float32(0.0)) + jnp.where(
        token_slots[:, 1:2] == slot_ids[None, :], flat_gates[:, 1:2], jnp.float32(0.0)
    )
    expert_mix = jnp.dot(
        combine, result_rows.astype(jnp.float32), precision=lax.Precision.HIGHEST,
        preferred_element_type=jnp.float32,
    ).reshape(local_images, tokens_dev, width)
    return (middle + expert_mix).astype(jnp.bfloat16)


def solution(mesh):
    placed = (
        P(("node", "ep"), None, None),
        P(None, "node"),
        P(None, "node"),
        P(None, "node"),
        P(),
        P(),
        P("ep", None, "node"),
        P("ep", "node", None),
        P(("node", "ep"), None, None),
    )
    return jax.shard_map(
        shards, mesh=mesh, in_specs=placed, out_specs=P(("node", "ep"), None, None), check_vma=False
    )
```

```python
import math

import jax
import jax.numpy as jnp
from jax import lax
from jax.sharding import PartitionSpec as P

D = 1280
HEADS = 16
CAP = 24
MOE_CHUNKS = 2


def layer_norm(values):
    center = values - jnp.mean(values, axis=-1, keepdims=True)
    spread = jnp.mean(center * center, axis=-1, keepdims=True)
    return center * lax.rsqrt(spread + 1e-06)


def slot_table(chosen, num_experts):
    onehot = (chosen[..., None] == jnp.arange(num_experts, dtype=jnp.int32)).astype(jnp.int32)
    before = jnp.cumsum(onehot, axis=1) - onehot
    return jnp.sum(before * onehot, axis=-1)


def shards(images, w_query, w_key, w_value, w_output, router, w_in, w_out, routes):
    local_images, tokens_dev, width = images.shape
    head_size = D // HEADS
    local_heads = w_query.shape[1] // head_size
    node_count = lax.axis_size("node")
    column_count = lax.axis_size("ep")
    num_experts = router.shape[1]
    local_experts = w_in.shape[0]
    slot_count = local_images * CAP
    inputs = images.astype(jnp.float32)
    normed = layer_norm(inputs).astype(jnp.bfloat16)
    node_index = lax.axis_index("node")
    ahead = [(i, (i + 1) % node_count) for i in range(node_count)]
    behind = [(i, (i - 1) % node_count) for i in range(node_count)]
    split = width // 2
    from_behind = lax.ppermute(normed, "node", ahead)
    from_ahead = lax.ppermute(normed, "node", behind)
    far = jnp.concatenate(
        [
            lax.ppermute(from_behind[..., :split], "node", ahead),
            lax.ppermute(from_ahead[..., split:], "node", behind),
        ],
        axis=-1,
    )
    shard_list = [normed, from_ahead, far, from_behind]
    number = len(shard_list)

    def project(weight):
        return jnp.concatenate(
            [
                jnp.einsum("ctd,de->cet", rows, weight, preferred_element_type=jnp.float32).astype(jnp.bfloat16)
                for rows in shard_list
            ],
            axis=0,
        )

    queries = project(w_query)
    projected_keys = project(w_key)
    projected_values = project(w_value)
    query_heads = queries.reshape(number, local_heads, head_size, tokens_dev)
    key_heads = projected_keys.reshape(number, local_heads, head_size, tokens_dev)
    value_heads = projected_values.reshape(number, local_heads, head_size, tokens_dev)
    scores = jnp.einsum(
        "chdq,chdk->chqk", query_heads, key_heads, preferred_element_type=jnp.float32
    ) / math.sqrt(head_size)
    weights = jax.nn.softmax(scores, axis=-1).astype(jnp.bfloat16)
    mixture = jnp.einsum(
        "chqk,chdk->cqhd", weights, value_heads, preferred_element_type=jnp.float32
    ).astype(jnp.bfloat16)
    head_results = jnp.roll(mixture.reshape(number, tokens_dev, local_heads * head_size), node_index, axis=0)
    exchanged = lax.all_to_all(head_results, "node", split_axis=0, concat_axis=0, tiled=True)
    attention = jnp.einsum(
        "gtd,gde->te",
        exchanged,
        w_output.reshape(node_count, local_heads * head_size, width),
        preferred_element_type=jnp.float32,
    ).reshape(local_images, tokens_dev, width)
    middle = inputs + attention
    normed_second = layer_norm(middle).astype(jnp.bfloat16)
    logits = jnp.einsum("itd,de->ite", normed_second, router, preferred_element_type=jnp.float32)
    chosen_mask = routes[..., None] == jnp.arange(num_experts, dtype=jnp.int32)
    chosen_logit = jnp.sum(jnp.where(chosen_mask, logits[:, :, None, :], jnp.float32(0.0)), axis=-1)
    gate_values = jax.nn.sigmoid(chosen_logit)
    flat_routes = routes.reshape(local_images, 2 * tokens_dev)
    slot_index = slot_table(flat_routes, num_experts)
    image_base = jnp.arange(local_images, dtype=jnp.int32)[:, None] * CAP
    position = (flat_routes * slot_count + image_base + slot_index).reshape(-1)
    token_count = local_images * tokens_dev
    token_slots = position.reshape(token_count, 2)
    slot_ids = jnp.arange(num_experts * slot_count, dtype=jnp.int32)
    token_rows = normed_second.reshape(token_count, width)
    hits = (token_slots[None, :, 0] == slot_ids[:, None]) | (token_slots[None, :, 1] == slot_ids[:, None])
    gathered = jnp.dot(
        hits.astype(jnp.bfloat16), token_rows, preferred_element_type=jnp.float32
    ).astype(jnp.bfloat16)
    outgoing = gathered.reshape(column_count, local_experts, slot_count, width)
    chunk = slot_count // MOE_CHUNKS
    pieces = []
    for part in range(MOE_CHUNKS):
        sent = outgoing[:, :, part * chunk:(part + 1) * chunk, :]
        block = lax.all_to_all(sent, "ep", split_axis=0, concat_axis=0, tiled=True).reshape(-1, width)
        half = block.shape[0] // 2
        came_behind = lax.ppermute(block, "node", ahead)
        came_ahead = lax.ppermute(block, "node", behind)
        came_far = jnp.concatenate(
            [
                lax.ppermute(came_behind[:half], "node", ahead),
                lax.ppermute(came_ahead[half:], "node", behind),
            ],
            axis=0,
        )
        rows = jnp.concatenate([block, came_ahead, came_far, came_behind], axis=0)
        pre_act = jnp.dot(rows, w_in[0], preferred_element_type=jnp.float32)
        hidden = jax.nn.gelu(pre_act, approximate=True).astype(jnp.bfloat16)
        partial_sum = jnp.dot(hidden, w_out[0], preferred_element_type=jnp.float32).astype(jnp.bfloat16)
        own_part, next_part, far_part, prev_part = jnp.split(partial_sum, node_count, axis=0)
        got_low = lax.ppermute(far_part[:half], "node", ahead).astype(jnp.float32)
        got_high = lax.ppermute(far_part[half:], "node", behind).astype(jnp.float32)
        to_next = jnp.concatenate(
            [next_part[:half].astype(jnp.float32) + got_low, next_part[half:].astype(jnp.float32)], axis=0
        )
        to_prev = jnp.concatenate(
            [prev_part[:half].astype(jnp.float32), prev_part[half:].astype(jnp.float32) + got_high], axis=0
        )
        back_behind = lax.ppermute(to_next.astype(jnp.bfloat16), "node", ahead)
        back_ahead = lax.ppermute(to_prev.astype(jnp.bfloat16), "node", behind)
        summed = (
            own_part.astype(jnp.float32) + back_behind.astype(jnp.float32) + back_ahead.astype(jnp.float32)
        ).astype(jnp.bfloat16)
        summed = summed.reshape(column_count, local_experts, chunk, width)
        pieces.append(lax.all_to_all(summed, "ep", split_axis=0, concat_axis=0, tiled=True))
    expert_result = jnp.concatenate(pieces, axis=2)
    result_rows = expert_result.reshape(num_experts * slot_count, width)
    flat_gates = gate_values.reshape(token_count, 2)
    combine = jnp.where(token_slots[:, 0:1] == slot_ids[None, :], flat_gates[:, 0:1], jnp.float32(0.0)) + jnp.where(
        token_slots[:, 1:2] == slot_ids[None, :], flat_gates[:, 1:2], jnp.float32(0.0)
    )
    expert_mix = jnp.dot(
        combine, result_rows.astype(jnp.float32), precision=lax.Precision.HIGHEST,
        preferred_element_type=jnp.float32,
    ).reshape(local_images, tokens_dev, width)
    return (middle + expert_mix).astype(jnp.bfloat16)


def solution(mesh):
    placed = (
        P(("node", "ep"), None, None),
        P(None, "node"),
        P(None, "node"),
        P(None, "node"),
        P(),
        P(),
        P("ep", None, "node"),
        P("ep", "node", None),
        P(("node", "ep"), None, None),
    )
    return jax.shard_map(
        shards, mesh=mesh, in_specs=placed, out_specs=P(("node", "ep"), None, None), check_vma=False
    )
```

```python
import math

import jax
import jax.numpy as jnp
from jax import lax
from jax.sharding import PartitionSpec as P

D = 1280
HEADS = 16
CAP = 24
MOE_CHUNKS = 2


def layer_norm(values):
    center = values - jnp.mean(values, axis=-1, keepdims=True)
    spread = jnp.mean(center * center, axis=-1, keepdims=True)
    return center * lax.rsqrt(spread + 1e-06)


def slot_table(chosen, num_experts):
    onehot = (chosen[..., None] == jnp.arange(num_experts, dtype=jnp.int32)).astype(jnp.int32)
    before = jnp.cumsum(onehot, axis=1) - onehot
    return jnp.sum(before * onehot, axis=-1)


def shards(images, w_query, w_key, w_value, w_output, router, w_in, w_out, routes):
    local_images, tokens_dev, width = images.shape
    head_size = D // HEADS
    local_heads = w_query.shape[1] // head_size
    node_count = lax.axis_size("node")
    column_count = lax.axis_size("ep")
    num_experts = router.shape[1]
    local_experts = w_in.shape[0]
    slot_count = local_images * CAP
    inputs = images.astype(jnp.float32)
    normed = layer_norm(inputs).astype(jnp.bfloat16)
    node_index = lax.axis_index("node")
    ahead = [(i, (i + 1) % node_count) for i in range(node_count)]
    behind = [(i, (i - 1) % node_count) for i in range(node_count)]
    split = width // 2
    from_behind = lax.ppermute(normed, "node", ahead)
    from_ahead = lax.ppermute(normed, "node", behind)
    far = jnp.concatenate(
        [
            lax.ppermute(from_behind[..., :split], "node", ahead),
            lax.ppermute(from_ahead[..., split:], "node", behind),
        ],
        axis=-1,
    )
    shard_rows = jnp.concatenate([normed, from_ahead, far, from_behind], axis=0)
    number = shard_rows.shape[0]
    queries = jnp.einsum(
        "ctd,de->cet", shard_rows, w_query, preferred_element_type=jnp.float32
    ).astype(jnp.bfloat16)
    projected_keys = jnp.einsum(
        "ctd,de->cet", shard_rows, w_key, preferred_element_type=jnp.float32
    ).astype(jnp.bfloat16)
    projected_values = jnp.einsum(
        "ctd,de->cet", shard_rows, w_value, preferred_element_type=jnp.float32
    ).astype(jnp.bfloat16)
    query_heads = queries.reshape(number, local_heads, head_size, tokens_dev)
    key_heads = projected_keys.reshape(number, local_heads, head_size, tokens_dev)
    value_heads = projected_values.reshape(number, local_heads, head_size, tokens_dev)
    scores = jnp.einsum(
        "chdq,chdk->chqk", query_heads, key_heads, preferred_element_type=jnp.float32
    ) / math.sqrt(head_size)
    weights = jax.nn.softmax(scores, axis=-1).astype(jnp.bfloat16)
    mixture = jnp.einsum(
        "chqk,chdk->cqhd", weights, value_heads, preferred_element_type=jnp.float32
    ).astype(jnp.bfloat16)
    head_results = mixture.reshape(number, tokens_dev, local_heads * head_size)
    sent_ahead = lax.ppermute(head_results[1:3], "node", ahead)
    sent_behind = lax.ppermute(head_results[3], "node", behind)
    sent_far = lax.ppermute(sent_ahead[1], "node", ahead)
    exchanged = jnp.roll(
        jnp.stack([head_results[0], sent_behind, sent_far, sent_ahead[0]], axis=0), node_index, axis=0
    )
    attention = jnp.einsum(
        "gtd,gde->te",
        exchanged,
        w_output.reshape(node_count, local_heads * head_size, width),
        preferred_element_type=jnp.float32,
    ).reshape(local_images, tokens_dev, width)
    middle = inputs + attention
    normed_second = layer_norm(middle).astype(jnp.bfloat16)
    logits = jnp.einsum("itd,de->ite", normed_second, router, preferred_element_type=jnp.float32)
    chosen_mask = routes[..., None] == jnp.arange(num_experts, dtype=jnp.int32)
    chosen_logit = jnp.sum(jnp.where(chosen_mask, logits[:, :, None, :], jnp.float32(0.0)), axis=-1)
    gate_values = jax.nn.sigmoid(chosen_logit)
    flat_routes = routes.reshape(local_images, 2 * tokens_dev)
    slot_index = slot_table(flat_routes, num_experts)
    image_base = jnp.arange(local_images, dtype=jnp.int32)[:, None] * CAP
    position = (flat_routes * slot_count + image_base + slot_index).reshape(-1)
    token_count = local_images * tokens_dev
    token_slots = position.reshape(token_count, 2)
    slot_ids = jnp.arange(num_experts * slot_count, dtype=jnp.int32)
    token_rows = normed_second.reshape(token_count, width)
    hits = (token_slots[None, :, 0] == slot_ids[:, None]) | (token_slots[None, :, 1] == slot_ids[:, None])
    gathered = jnp.dot(
        hits.astype(jnp.bfloat16), token_rows, preferred_element_type=jnp.float32
    ).astype(jnp.bfloat16)
    outgoing = gathered.reshape(column_count, local_experts, slot_count, width)
    chunk = slot_count // MOE_CHUNKS
    pieces = []
    for part in range(MOE_CHUNKS):
        sent = outgoing[:, :, part * chunk:(part + 1) * chunk, :]
        block = lax.all_to_all(sent, "ep", split_axis=0, concat_axis=0, tiled=True).reshape(-1, width)
        half = block.shape[0] // 2
        came_behind = lax.ppermute(block, "node", ahead)
        came_ahead = lax.ppermute(block, "node", behind)
        came_far = jnp.concatenate(
            [
                lax.ppermute(came_behind[:half], "node", ahead),
                lax.ppermute(came_ahead[half:], "node", behind),
            ],
            axis=0,
        )
        rows = jnp.concatenate([block, came_ahead, came_far, came_behind], axis=0)
        pre_act = jnp.dot(rows, w_in[0], preferred_element_type=jnp.float32)
        hidden = jax.nn.gelu(pre_act, approximate=True).astype(jnp.bfloat16)
        partial_sum = jnp.dot(hidden, w_out[0], preferred_element_type=jnp.float32).astype(jnp.bfloat16)
        own_part, next_part, far_part, prev_part = jnp.split(partial_sum, node_count, axis=0)
        got_low = lax.ppermute(far_part[:half], "node", ahead).astype(jnp.float32)
        got_high = lax.ppermute(far_part[half:], "node", behind).astype(jnp.float32)
        to_next = jnp.concatenate(
            [next_part[:half].astype(jnp.float32) + got_low, next_part[half:].astype(jnp.float32)], axis=0
        )
        to_prev = jnp.concatenate(
            [prev_part[:half].astype(jnp.float32), prev_part[half:].astype(jnp.float32) + got_high], axis=0
        )
        back_behind = lax.ppermute(to_next.astype(jnp.bfloat16), "node", ahead)
        back_ahead = lax.ppermute(to_prev.astype(jnp.bfloat16), "node", behind)
        summed = (
            own_part.astype(jnp.float32) + back_behind.astype(jnp.float32) + back_ahead.astype(jnp.float32)
        ).astype(jnp.bfloat16)
        summed = summed.reshape(column_count, local_experts, chunk, width)
        pieces.append(lax.all_to_all(summed, "ep", split_axis=0, concat_axis=0, tiled=True))
    expert_result = jnp.concatenate(pieces, axis=2)
    result_rows = expert_result.reshape(num_experts * slot_count, width)
    flat_gates = gate_values.reshape(token_count, 2)
    combine = jnp.where(token_slots[:, 0:1] == slot_ids[None, :], flat_gates[:, 0:1], jnp.float32(0.0)) + jnp.where(
        token_slots[:, 1:2] == slot_ids[None, :], flat_gates[:, 1:2], jnp.float32(0.0)
    )
    expert_mix = jnp.dot(
        combine, result_rows.astype(jnp.float32), precision=lax.Precision.HIGHEST,
        preferred_element_type=jnp.float32,
    ).reshape(local_images, tokens_dev, width)
    return (middle + expert_mix).astype(jnp.bfloat16)


def solution(mesh):
    placed = (
        P(("node", "ep"), None, None),
        P(None, "node"),
        P(None, "node"),
        P(None, "node"),
        P(),
        P(),
        P("ep", None, "node"),
        P("ep", "node", None),
        P(("node", "ep"), None, None),
    )
    return jax.shard_map(
        shards, mesh=mesh, in_specs=placed, out_specs=P(("node", "ep"), None, None), check_vma=False
    )
```

```python
import math

import jax
import jax.numpy as jnp
from jax import lax
from jax.sharding import PartitionSpec as P

D = 1280
HEADS = 16
CAP = 24


def layer_norm(values):
    center = values - jnp.mean(values, axis=-1, keepdims=True)
    spread = jnp.mean(center * center, axis=-1, keepdims=True)
    return center * lax.rsqrt(spread + 1e-06)


def slot_table(chosen, num_experts):
    onehot = (chosen[..., None] == jnp.arange(num_experts, dtype=jnp.int32)).astype(jnp.int32)
    before = jnp.cumsum(onehot, axis=1) - onehot
    return jnp.sum(before * onehot, axis=-1)


def shards(images, w_query, w_key, w_value, w_output, router, w_in, w_out, routes):
    local_images, tokens_dev, width = images.shape
    head_size = D // HEADS
    local_heads = w_query.shape[1] // head_size
    node_count = lax.axis_size("node")
    column_count = lax.axis_size("ep")
    num_experts = router.shape[1]
    local_experts = w_in.shape[0]
    slot_count = local_images * CAP
    inputs = images.astype(jnp.float32)
    normed = layer_norm(inputs).astype(jnp.bfloat16)
    node_index = lax.axis_index("node")
    ahead = [(i, (i + 1) % node_count) for i in range(node_count)]
    behind = [(i, (i - 1) % node_count) for i in range(node_count)]
    split = width // 2
    from_behind = lax.ppermute(normed, "node", ahead)
    from_ahead = lax.ppermute(normed, "node", behind)
    far = jnp.concatenate(
        [
            lax.ppermute(from_behind[..., :split], "node", ahead),
            lax.ppermute(from_ahead[..., split:], "node", behind),
        ],
        axis=-1,
    )
    shard_rows = jnp.concatenate([normed, from_ahead, far, from_behind], axis=0)
    number = shard_rows.shape[0]
    queries = jnp.einsum(
        "ctd,de->cet", shard_rows, w_query, preferred_element_type=jnp.float32
    ).astype(jnp.bfloat16)
    projected_keys = jnp.einsum(
        "ctd,de->cet", shard_rows, w_key, preferred_element_type=jnp.float32
    ).astype(jnp.bfloat16)
    projected_values = jnp.einsum(
        "ctd,de->cet", shard_rows, w_value, preferred_element_type=jnp.float32
    ).astype(jnp.bfloat16)
    query_heads = queries.reshape(number, local_heads, head_size, tokens_dev)
    key_heads = projected_keys.reshape(number, local_heads, head_size, tokens_dev)
    value_heads = projected_values.reshape(number, local_heads, head_size, tokens_dev)
    scores = jnp.einsum(
        "chdq,chdk->chqk", query_heads, key_heads, preferred_element_type=jnp.float32
    ) / math.sqrt(head_size)
    weights = jax.nn.softmax(scores, axis=-1).astype(jnp.bfloat16)
    mixture = jnp.einsum(
        "chqk,chdk->cqhd", weights, value_heads, preferred_element_type=jnp.float32
    ).astype(jnp.bfloat16)
    head_results = jnp.roll(mixture.reshape(number, tokens_dev, local_heads * head_size), node_index, axis=0)
    exchanged = lax.all_to_all(head_results, "node", split_axis=0, concat_axis=0, tiled=True)
    attention = jnp.einsum(
        "gtd,gde->te",
        exchanged,
        w_output.reshape(node_count, local_heads * head_size, width),
        preferred_element_type=jnp.float32,
    ).reshape(local_images, tokens_dev, width)
    middle = inputs + attention
    normed_second = layer_norm(middle).astype(jnp.bfloat16)
    logits = jnp.einsum("itd,de->ite", normed_second, router, preferred_element_type=jnp.float32)
    chosen_mask = routes[..., None] == jnp.arange(num_experts, dtype=jnp.int32)
    chosen_logit = jnp.sum(jnp.where(chosen_mask, logits[:, :, None, :], jnp.float32(0.0)), axis=-1)
    gate_values = jax.nn.sigmoid(chosen_logit)
    flat_routes = routes.reshape(local_images, 2 * tokens_dev)
    slot_index = slot_table(flat_routes, num_experts)
    image_base = jnp.arange(local_images, dtype=jnp.int32)[:, None] * CAP
    position = (flat_routes * slot_count + image_base + slot_index).reshape(-1)
    token_count = local_images * tokens_dev
    token_slots = position.reshape(token_count, 2)
    slot_ids = jnp.arange(num_experts * slot_count, dtype=jnp.int32)
    token_rows = normed_second.reshape(token_count, width)
    hits = (token_slots[None, :, 0] == slot_ids[:, None]) | (token_slots[None, :, 1] == slot_ids[:, None])
    gathered = jnp.dot(
        hits.astype(jnp.bfloat16), token_rows, preferred_element_type=jnp.float32
    ).astype(jnp.bfloat16)
    outgoing = gathered.reshape(column_count, local_experts, slot_count, width)
    bounds = [0, slot_count // 3, slot_count]
    pieces = []
    for low, high in zip(bounds[:-1], bounds[1:]):
        chunk = high - low
        sent = outgoing[:, :, low:high, :]
        block = lax.all_to_all(sent, "ep", split_axis=0, concat_axis=0, tiled=True).reshape(-1, width)
        half = block.shape[0] // 2
        came_behind = lax.ppermute(block, "node", ahead)
        came_ahead = lax.ppermute(block, "node", behind)
        came_far = jnp.concatenate(
            [
                lax.ppermute(came_behind[:half], "node", ahead),
                lax.ppermute(came_ahead[half:], "node", behind),
            ],
            axis=0,
        )
        rows = jnp.concatenate([block, came_ahead, came_far, came_behind], axis=0)
        pre_act = jnp.dot(rows, w_in[0], preferred_element_type=jnp.float32)
        hidden = jax.nn.gelu(pre_act, approximate=True).astype(jnp.bfloat16)
        partial_sum = jnp.dot(hidden, w_out[0], preferred_element_type=jnp.float32).astype(jnp.bfloat16)
        own_part, next_part, far_part, prev_part = jnp.split(partial_sum, node_count, axis=0)
        got_low = lax.ppermute(far_part[:half], "node", ahead).astype(jnp.float32)
        got_high = lax.ppermute(far_part[half:], "node", behind).astype(jnp.float32)
        to_next = jnp.concatenate(
            [next_part[:half].astype(jnp.float32) + got_low, next_part[half:].astype(jnp.float32)], axis=0
        )
        to_prev = jnp.concatenate(
            [prev_part[:half].astype(jnp.float32), prev_part[half:].astype(jnp.float32) + got_high], axis=0
        )
        back_behind = lax.ppermute(to_next.astype(jnp.bfloat16), "node", ahead)
        back_ahead = lax.ppermute(to_prev.astype(jnp.bfloat16), "node", behind)
        summed = (
            own_part.astype(jnp.float32) + back_behind.astype(jnp.float32) + back_ahead.astype(jnp.float32)
        ).astype(jnp.bfloat16)
        summed = summed.reshape(column_count, local_experts, chunk, width)
        pieces.append(lax.all_to_all(summed, "ep", split_axis=0, concat_axis=0, tiled=True))
    expert_result = jnp.concatenate(pieces, axis=2)
    result_rows = expert_result.reshape(num_experts * slot_count, width)
    flat_gates = gate_values.reshape(token_count, 2)
    combine = jnp.where(token_slots[:, 0:1] == slot_ids[None, :], flat_gates[:, 0:1], jnp.float32(0.0)) + jnp.where(
        token_slots[:, 1:2] == slot_ids[None, :], flat_gates[:, 1:2], jnp.float32(0.0)
    )
    expert_mix = jnp.dot(
        combine, result_rows.astype(jnp.float32), precision=lax.Precision.HIGHEST,
        preferred_element_type=jnp.float32,
    ).reshape(local_images, tokens_dev, width)
    return (middle + expert_mix).astype(jnp.bfloat16)


def solution(mesh):
    placed = (
        P(("node", "ep"), None, None),
        P(None, "node"),
        P(None, "node"),
        P(None, "node"),
        P(),
        P(),
        P("ep", None, "node"),
        P("ep", "node", None),
        P(("node", "ep"), None, None),
    )
    return jax.shard_map(
        shards, mesh=mesh, in_specs=placed, out_specs=P(("node", "ep"), None, None), check_vma=False
    )
```

```python
import math

import jax
import jax.numpy as jnp
from jax import lax
from jax.sharding import PartitionSpec as P

D = 1280
HEADS = 16
CAP = 24
MOE_CHUNKS = 2


def layer_norm(values):
    center = values - jnp.mean(values, axis=-1, keepdims=True)
    spread = jnp.mean(center * center, axis=-1, keepdims=True)
    return center * lax.rsqrt(spread + 1e-06)


def slot_table(chosen, num_experts):
    onehot = (chosen[..., None] == jnp.arange(num_experts, dtype=jnp.int32)).astype(jnp.int32)
    before = jnp.cumsum(onehot, axis=1) - onehot
    return jnp.sum(before * onehot, axis=-1)


def shards(images, w_query, w_key, w_value, w_output, router, w_in, w_out, routes):
    local_images, tokens_dev, width = images.shape
    head_size = D // HEADS
    local_heads = w_query.shape[1] // head_size
    node_count = lax.axis_size("node")
    column_count = lax.axis_size("ep")
    num_experts = router.shape[1]
    local_experts = w_in.shape[0]
    slot_count = local_images * CAP
    inputs = images.astype(jnp.float32)
    normed = layer_norm(inputs).astype(jnp.bfloat16)
    node_index = lax.axis_index("node")
    ahead = [(i, (i + 1) % node_count) for i in range(node_count)]
    behind = [(i, (i - 1) % node_count) for i in range(node_count)]
    split = width // 2
    from_behind = lax.ppermute(normed, "node", ahead)
    from_ahead = lax.ppermute(normed, "node", behind)
    far = jnp.concatenate(
        [
            lax.ppermute(from_behind[..., :split], "node", ahead),
            lax.ppermute(from_ahead[..., split:], "node", behind),
        ],
        axis=-1,
    )
    shard_rows = jnp.concatenate([normed, from_ahead, far, from_behind], axis=0)
    number = shard_rows.shape[0]
    queries = jnp.einsum(
        "ctd,de->cet", shard_rows, w_query, preferred_element_type=jnp.float32
    ).astype(jnp.bfloat16)
    projected_keys = jnp.einsum(
        "ctd,de->cet", shard_rows, w_key, preferred_element_type=jnp.float32
    ).astype(jnp.bfloat16)
    projected_values = jnp.einsum(
        "ctd,de->cet", shard_rows, w_value, preferred_element_type=jnp.float32
    ).astype(jnp.bfloat16)
    query_heads = queries.reshape(number, local_heads, head_size, tokens_dev)
    key_heads = projected_keys.reshape(number, local_heads, head_size, tokens_dev)
    value_heads = projected_values.reshape(number, local_heads, head_size, tokens_dev)
    scores = jnp.einsum(
        "chdq,chdk->chqk", query_heads, key_heads, preferred_element_type=jnp.float32
    ) / math.sqrt(head_size)
    weights = jax.nn.softmax(scores, axis=-1).astype(jnp.bfloat16)
    mixture = jnp.einsum(
        "chqk,chdk->cqhd", weights, value_heads, preferred_element_type=jnp.float32
    ).astype(jnp.bfloat16)
    head_results = jnp.roll(mixture.reshape(number, tokens_dev, local_heads * head_size), node_index, axis=0)
    exchanged = lax.all_to_all(head_results, "node", split_axis=0, concat_axis=0, tiled=True)
    attention = jnp.einsum(
        "gtd,gde->te",
        exchanged,
        w_output.reshape(node_count, local_heads * head_size, width),
        preferred_element_type=jnp.float32,
    ).reshape(local_images, tokens_dev, width)
    middle = inputs + attention
    normed_second = layer_norm(middle).astype(jnp.bfloat16)
    logits = jnp.einsum("itd,de->ite", normed_second, router, preferred_element_type=jnp.float32)
    chosen_mask = routes[..., None] == jnp.arange(num_experts, dtype=jnp.int32)
    chosen_logit = jnp.sum(jnp.where(chosen_mask, logits[:, :, None, :], jnp.float32(0.0)), axis=-1)
    gate_values = jax.nn.sigmoid(chosen_logit)
    flat_routes = routes.reshape(local_images, 2 * tokens_dev)
    slot_index = slot_table(flat_routes, num_experts)
    image_base = jnp.arange(local_images, dtype=jnp.int32)[:, None] * CAP
    position = (flat_routes * slot_count + image_base + slot_index).reshape(-1)
    token_count = local_images * tokens_dev
    token_slots = position.reshape(token_count, 2)
    slot_ids = jnp.arange(num_experts * slot_count, dtype=jnp.int32)
    token_rows = normed_second.reshape(token_count, width)
    hits = (token_slots[None, :, 0] == slot_ids[:, None]) | (token_slots[None, :, 1] == slot_ids[:, None])
    gathered = jnp.dot(
        hits.astype(jnp.bfloat16), token_rows, preferred_element_type=jnp.float32
    ).astype(jnp.bfloat16)
    outgoing = gathered.reshape(column_count, local_experts, slot_count, width)
    chunk = slot_count // MOE_CHUNKS
    pieces = []
    for part in range(MOE_CHUNKS):
        sent = outgoing[:, :, part * chunk:(part + 1) * chunk, :]
        block = lax.all_to_all(sent, "ep", split_axis=0, concat_axis=0, tiled=True).reshape(-1, width)
        half = block.shape[0] // 2
        came_behind = lax.ppermute(block, "node", ahead)
        came_ahead = lax.ppermute(block, "node", behind)
        came_far = jnp.concatenate(
            [
                lax.ppermute(came_behind[:half], "node", ahead),
                lax.ppermute(came_ahead[half:], "node", behind),
            ],
            axis=0,
        )
        rows = jnp.concatenate([block, came_ahead, came_far, came_behind], axis=0)
        pre_act = jnp.dot(rows, w_in[0], preferred_element_type=jnp.float32)
        hidden = jax.nn.gelu(pre_act, approximate=True).astype(jnp.bfloat16)
        partial_sum = jnp.dot(hidden, w_out[0], preferred_element_type=jnp.float32).astype(jnp.bfloat16)
        own_part, next_part, far_part, prev_part = jnp.split(partial_sum, node_count, axis=0)
        got_low = lax.ppermute(far_part[:half], "node", ahead).astype(jnp.float32)
        got_high = lax.ppermute(far_part[half:], "node", behind).astype(jnp.float32)
        to_next = jnp.concatenate(
            [next_part[:half].astype(jnp.float32) + got_low, next_part[half:].astype(jnp.float32)], axis=0
        )
        to_prev = jnp.concatenate(
            [prev_part[:half].astype(jnp.float32), prev_part[half:].astype(jnp.float32) + got_high], axis=0
        )
        back_behind = lax.ppermute(to_next.astype(jnp.bfloat16), "node", ahead)
        back_ahead = lax.ppermute(to_prev.astype(jnp.bfloat16), "node", behind)
        summed = (
            own_part.astype(jnp.float32) + back_behind.astype(jnp.float32) + back_ahead.astype(jnp.float32)
        ).astype(jnp.bfloat16)
        summed = summed.reshape(column_count, local_experts, chunk, width)
        pieces.append(lax.all_to_all(summed, "ep", split_axis=0, concat_axis=0, tiled=True))
    flat_gates = gate_values.reshape(token_count, 2)
    chunk = slot_count // MOE_CHUNKS
    expert_mix = jnp.zeros((token_count, width), jnp.float32)
    for part, piece in enumerate(pieces):
        piece_ids = (
            jnp.arange(num_experts, dtype=jnp.int32)[:, None] * slot_count
            + jnp.arange(part * chunk, (part + 1) * chunk, dtype=jnp.int32)[None, :]
        ).reshape(-1)
        combine = jnp.where(
            token_slots[:, 0:1] == piece_ids[None, :], flat_gates[:, 0:1], jnp.float32(0.0)
        ) + jnp.where(token_slots[:, 1:2] == piece_ids[None, :], flat_gates[:, 1:2], jnp.float32(0.0))
        expert_mix = expert_mix + jnp.dot(
            combine, piece.reshape(-1, width).astype(jnp.float32), precision=lax.Precision.HIGHEST,
            preferred_element_type=jnp.float32,
        )
    expert_mix = expert_mix.reshape(local_images, tokens_dev, width)
    return (middle + expert_mix).astype(jnp.bfloat16)


def solution(mesh):
    placed = (
        P(("node", "ep"), None, None),
        P(None, "node"),
        P(None, "node"),
        P(None, "node"),
        P(),
        P(),
        P("ep", None, "node"),
        P("ep", "node", None),
        P(("node", "ep"), None, None),
    )
    return jax.shard_map(
        shards, mesh=mesh, in_specs=placed, out_specs=P(("node", "ep"), None, None), check_vma=False
    )
```

```python
import math

import jax
import jax.numpy as jnp
from jax import lax
from jax.sharding import PartitionSpec as P

D = 1280
HEADS = 16
CAP = 24
MOE_CHUNKS = 2


def layer_norm(values):
    center = values - jnp.mean(values, axis=-1, keepdims=True)
    spread = jnp.mean(center * center, axis=-1, keepdims=True)
    return center * lax.rsqrt(spread + 1e-06)


def slot_table(chosen, num_experts):
    onehot = (chosen[..., None] == jnp.arange(num_experts, dtype=jnp.int32)).astype(jnp.int32)
    before = jnp.cumsum(onehot, axis=1) - onehot
    return jnp.sum(before * onehot, axis=-1)


def shards(images, w_query, w_key, w_value, w_output, router, w_in, w_out, routes):
    local_images, tokens_dev, width = images.shape
    head_size = D // HEADS
    local_heads = w_query.shape[1] // head_size
    node_count = lax.axis_size("node")
    column_count = lax.axis_size("ep")
    num_experts = router.shape[1]
    local_experts = w_in.shape[0]
    slot_count = local_images * CAP
    inputs = images.astype(jnp.float32)
    normed = layer_norm(inputs).astype(jnp.bfloat16)
    node_index = lax.axis_index("node")
    ahead = [(i, (i + 1) % node_count) for i in range(node_count)]
    behind = [(i, (i - 1) % node_count) for i in range(node_count)]
    split = width // 2
    from_behind = lax.ppermute(normed, "node", ahead)
    from_ahead = lax.ppermute(normed, "node", behind)
    far = jnp.concatenate(
        [
            lax.ppermute(from_behind[..., :split], "node", ahead),
            lax.ppermute(from_ahead[..., split:], "node", behind),
        ],
        axis=-1,
    )
    shard_rows = jnp.concatenate([normed, from_ahead, far, from_behind], axis=0)
    number = shard_rows.shape[0]
    queries = jnp.einsum(
        "ctd,de->cet", shard_rows, w_query, preferred_element_type=jnp.float32
    ).astype(jnp.bfloat16)
    projected_keys = jnp.einsum(
        "ctd,de->cet", shard_rows, w_key, preferred_element_type=jnp.float32
    ).astype(jnp.bfloat16)
    projected_values = jnp.einsum(
        "ctd,de->cet", shard_rows, w_value, preferred_element_type=jnp.float32
    ).astype(jnp.bfloat16)
    query_heads = queries.reshape(number, local_heads, head_size, tokens_dev)
    key_heads = projected_keys.reshape(number, local_heads, head_size, tokens_dev)
    value_heads = projected_values.reshape(number, local_heads, head_size, tokens_dev)
    scores = jnp.einsum(
        "chdq,chdk->chqk", query_heads, key_heads, preferred_element_type=jnp.float32
    ) / math.sqrt(head_size)
    weights = jax.nn.softmax(scores, axis=-1).astype(jnp.bfloat16)
    mixture = jnp.einsum(
        "chqk,chdk->cqhd", weights, value_heads, preferred_element_type=jnp.float32
    ).astype(jnp.bfloat16)
    head_results = jnp.roll(mixture.reshape(number, tokens_dev, local_heads * head_size), node_index, axis=0)
    exchanged = lax.all_to_all(head_results, "node", split_axis=0, concat_axis=0, tiled=True)
    attention = jnp.einsum(
        "gtd,gde->te",
        exchanged,
        w_output.reshape(node_count, local_heads * head_size, width),
        preferred_element_type=jnp.float32,
    ).reshape(local_images, tokens_dev, width)
    middle = inputs + attention
    normed_second = layer_norm(middle).astype(jnp.bfloat16)
    logits = jnp.einsum("itd,de->ite", normed_second, router, preferred_element_type=jnp.float32)
    chosen_mask = routes[..., None] == jnp.arange(num_experts, dtype=jnp.int32)
    chosen_logit = jnp.sum(jnp.where(chosen_mask, logits[:, :, None, :], jnp.float32(0.0)), axis=-1)
    gate_values = jax.nn.sigmoid(chosen_logit)
    flat_routes = routes.reshape(local_images, 2 * tokens_dev)
    slot_index = slot_table(flat_routes, num_experts)
    image_base = jnp.arange(local_images, dtype=jnp.int32)[:, None] * CAP
    position = (flat_routes * slot_count + image_base + slot_index).reshape(-1)
    token_count = local_images * tokens_dev
    token_slots = position.reshape(token_count, 2)
    slot_ids = jnp.arange(num_experts * slot_count, dtype=jnp.int32)
    token_rows = normed_second.reshape(token_count, width)
    hits = (token_slots[None, :, 0] == slot_ids[:, None]) | (token_slots[None, :, 1] == slot_ids[:, None])
    gathered = jnp.dot(
        hits.astype(jnp.bfloat16), token_rows, preferred_element_type=jnp.float32
    ).astype(jnp.bfloat16)
    outgoing = gathered.reshape(column_count, local_experts, slot_count, width)
    chunk = slot_count // MOE_CHUNKS
    pieces = []
    for part in range(MOE_CHUNKS):
        sent = outgoing[:, :, part * chunk:(part + 1) * chunk, :]
        block = lax.all_to_all(sent, "ep", split_axis=0, concat_axis=0, tiled=True).reshape(-1, width)
        half = block.shape[0] // 2
        came_behind = lax.ppermute(block, "node", ahead)
        came_ahead = lax.ppermute(block, "node", behind)
        if part % 2 == 0:
            came_far = lax.ppermute(came_behind, "node", ahead)
        else:
            came_far = lax.ppermute(came_ahead, "node", behind)
        rows = jnp.concatenate([block, came_ahead, came_far, came_behind], axis=0)
        pre_act = jnp.dot(rows, w_in[0], preferred_element_type=jnp.float32)
        hidden = jax.nn.gelu(pre_act, approximate=True).astype(jnp.bfloat16)
        partial_sum = jnp.dot(hidden, w_out[0], preferred_element_type=jnp.float32).astype(jnp.bfloat16)
        own_part, next_part, far_part, prev_part = jnp.split(partial_sum, node_count, axis=0)
        to_next = next_part.astype(jnp.float32)
        to_prev = prev_part.astype(jnp.float32)
        if part % 2 == 0:
            to_next = to_next + lax.ppermute(far_part, "node", ahead).astype(jnp.float32)
        else:
            to_prev = to_prev + lax.ppermute(far_part, "node", behind).astype(jnp.float32)
        back_behind = lax.ppermute(to_next.astype(jnp.bfloat16), "node", ahead)
        back_ahead = lax.ppermute(to_prev.astype(jnp.bfloat16), "node", behind)
        summed = (
            own_part.astype(jnp.float32) + back_behind.astype(jnp.float32) + back_ahead.astype(jnp.float32)
        ).astype(jnp.bfloat16)
        summed = summed.reshape(column_count, local_experts, chunk, width)
        pieces.append(lax.all_to_all(summed, "ep", split_axis=0, concat_axis=0, tiled=True))
    expert_result = jnp.concatenate(pieces, axis=2)
    result_rows = expert_result.reshape(num_experts * slot_count, width)
    flat_gates = gate_values.reshape(token_count, 2)
    combine = jnp.where(token_slots[:, 0:1] == slot_ids[None, :], flat_gates[:, 0:1], jnp.float32(0.0)) + jnp.where(
        token_slots[:, 1:2] == slot_ids[None, :], flat_gates[:, 1:2], jnp.float32(0.0)
    )
    expert_mix = jnp.dot(
        combine, result_rows.astype(jnp.float32), precision=lax.Precision.HIGHEST,
        preferred_element_type=jnp.float32,
    ).reshape(local_images, tokens_dev, width)
    return (middle + expert_mix).astype(jnp.bfloat16)


def solution(mesh):
    placed = (
        P(("node", "ep"), None, None),
        P(None, "node"),
        P(None, "node"),
        P(None, "node"),
        P(),
        P(),
        P("ep", None, "node"),
        P("ep", "node", None),
        P(("node", "ep"), None, None),
    )
    return jax.shard_map(
        shards, mesh=mesh, in_specs=placed, out_specs=P(("node", "ep"), None, None), check_vma=False
    )
```

```python
import math

import jax
import jax.numpy as jnp
from jax import lax
from jax.sharding import PartitionSpec as P

D = 1280
HEADS = 16
CAP = 24


def layer_norm(values):
    center = values - jnp.mean(values, axis=-1, keepdims=True)
    spread = jnp.mean(center * center, axis=-1, keepdims=True)
    return center * lax.rsqrt(spread + 1e-06)


def slot_table(chosen, num_experts):
    onehot = (chosen[..., None] == jnp.arange(num_experts, dtype=jnp.int32)).astype(jnp.int32)
    before = jnp.cumsum(onehot, axis=1) - onehot
    return jnp.sum(before * onehot, axis=-1)


def shards(images, w_query, w_key, w_value, w_output, router, w_in, w_out, routes):
    local_images, tokens_dev, width = images.shape
    head_size = D // HEADS
    local_heads = w_query.shape[1] // head_size
    node_count = lax.axis_size("node")
    column_count = lax.axis_size("ep")
    num_experts = router.shape[1]
    local_experts = w_in.shape[0]
    slot_count = local_images * CAP
    inputs = images.astype(jnp.float32)
    normed = layer_norm(inputs).astype(jnp.bfloat16)
    node_index = lax.axis_index("node")
    ahead = [(i, (i + 1) % node_count) for i in range(node_count)]
    behind = [(i, (i - 1) % node_count) for i in range(node_count)]
    split = width // 2
    from_behind = lax.ppermute(normed, "node", ahead)
    from_ahead = lax.ppermute(normed, "node", behind)
    far = jnp.concatenate(
        [
            lax.ppermute(from_behind[..., :split], "node", ahead),
            lax.ppermute(from_ahead[..., split:], "node", behind),
        ],
        axis=-1,
    )
    shard_rows = jnp.concatenate([normed, from_ahead, far, from_behind], axis=0)
    number = shard_rows.shape[0]
    queries = jnp.einsum(
        "ctd,de->cet", shard_rows, w_query, preferred_element_type=jnp.float32
    ).astype(jnp.bfloat16)
    projected_keys = jnp.einsum(
        "ctd,de->cet", shard_rows, w_key, preferred_element_type=jnp.float32
    ).astype(jnp.bfloat16)
    projected_values = jnp.einsum(
        "ctd,de->cet", shard_rows, w_value, preferred_element_type=jnp.float32
    ).astype(jnp.bfloat16)
    query_heads = queries.reshape(number, local_heads, head_size, tokens_dev)
    key_heads = projected_keys.reshape(number, local_heads, head_size, tokens_dev)
    value_heads = projected_values.reshape(number, local_heads, head_size, tokens_dev)
    scores = jnp.einsum(
        "chdq,chdk->chqk", query_heads, key_heads, preferred_element_type=jnp.float32
    ) / math.sqrt(head_size)
    weights = jax.nn.softmax(scores, axis=-1).astype(jnp.bfloat16)
    mixture = jnp.einsum(
        "chqk,chdk->cqhd", weights, value_heads, preferred_element_type=jnp.float32
    ).astype(jnp.bfloat16)
    head_results = jnp.roll(mixture.reshape(number, tokens_dev, local_heads * head_size), node_index, axis=0)
    exchanged = lax.all_to_all(head_results, "node", split_axis=0, concat_axis=0, tiled=True)
    attention = jnp.einsum(
        "gtd,gde->te",
        exchanged,
        w_output.reshape(node_count, local_heads * head_size, width),
        preferred_element_type=jnp.float32,
    ).reshape(local_images, tokens_dev, width)
    middle = inputs + attention
    normed_second = layer_norm(middle).astype(jnp.bfloat16)
    logits = jnp.einsum("itd,de->ite", normed_second, router, preferred_element_type=jnp.float32)
    chosen_mask = routes[..., None] == jnp.arange(num_experts, dtype=jnp.int32)
    chosen_logit = jnp.sum(jnp.where(chosen_mask, logits[:, :, None, :], jnp.float32(0.0)), axis=-1)
    gate_values = jax.nn.sigmoid(chosen_logit)
    flat_routes = routes.reshape(local_images, 2 * tokens_dev)
    slot_index = slot_table(flat_routes, num_experts)
    image_base = jnp.arange(local_images, dtype=jnp.int32)[:, None] * CAP
    position = (flat_routes * slot_count + image_base + slot_index).reshape(-1)
    token_count = local_images * tokens_dev
    token_slots = position.reshape(token_count, 2)
    slot_ids = jnp.arange(num_experts * slot_count, dtype=jnp.int32)
    token_rows = normed_second.reshape(token_count, width)
    hits = (token_slots[None, :, 0] == slot_ids[:, None]) | (token_slots[None, :, 1] == slot_ids[:, None])
    gathered = jnp.dot(
        hits.astype(jnp.bfloat16), token_rows, preferred_element_type=jnp.float32
    ).astype(jnp.bfloat16)
    outgoing = gathered.reshape(column_count, local_experts, slot_count, width)
    bounds = [0, 2 * slot_count // 3, slot_count]
    pieces = []
    for low, high in zip(bounds[:-1], bounds[1:]):
        chunk = high - low
        sent = outgoing[:, :, low:high, :]
        block = lax.all_to_all(sent, "ep", split_axis=0, concat_axis=0, tiled=True).reshape(-1, width)
        half = block.shape[0] // 2
        came_behind = lax.ppermute(block, "node", ahead)
        came_ahead = lax.ppermute(block, "node", behind)
        came_far = jnp.concatenate(
            [
                lax.ppermute(came_behind[:half], "node", ahead),
                lax.ppermute(came_ahead[half:], "node", behind),
            ],
            axis=0,
        )
        rows = jnp.concatenate([block, came_ahead, came_far, came_behind], axis=0)
        pre_act = jnp.dot(rows, w_in[0], preferred_element_type=jnp.float32)
        hidden = jax.nn.gelu(pre_act, approximate=True).astype(jnp.bfloat16)
        partial_sum = jnp.dot(hidden, w_out[0], preferred_element_type=jnp.float32).astype(jnp.bfloat16)
        own_part, next_part, far_part, prev_part = jnp.split(partial_sum, node_count, axis=0)
        got_low = lax.ppermute(far_part[:half], "node", ahead).astype(jnp.float32)
        got_high = lax.ppermute(far_part[half:], "node", behind).astype(jnp.float32)
        to_next = jnp.concatenate(
            [next_part[:half].astype(jnp.float32) + got_low, next_part[half:].astype(jnp.float32)], axis=0
        )
        to_prev = jnp.concatenate(
            [prev_part[:half].astype(jnp.float32), prev_part[half:].astype(jnp.float32) + got_high], axis=0
        )
        back_behind = lax.ppermute(to_next.astype(jnp.bfloat16), "node", ahead)
        back_ahead = lax.ppermute(to_prev.astype(jnp.bfloat16), "node", behind)
        summed = (
            own_part.astype(jnp.float32) + back_behind.astype(jnp.float32) + back_ahead.astype(jnp.float32)
        ).astype(jnp.bfloat16)
        summed = summed.reshape(column_count, local_experts, chunk, width)
        pieces.append(lax.all_to_all(summed, "ep", split_axis=0, concat_axis=0, tiled=True))
    expert_result = jnp.concatenate(pieces, axis=2)
    result_rows = expert_result.reshape(num_experts * slot_count, width)
    flat_gates = gate_values.reshape(token_count, 2)
    combine = jnp.where(token_slots[:, 0:1] == slot_ids[None, :], flat_gates[:, 0:1], jnp.float32(0.0)) + jnp.where(
        token_slots[:, 1:2] == slot_ids[None, :], flat_gates[:, 1:2], jnp.float32(0.0)
    )
    expert_mix = jnp.dot(
        combine, result_rows.astype(jnp.float32), precision=lax.Precision.HIGHEST,
        preferred_element_type=jnp.float32,
    ).reshape(local_images, tokens_dev, width)
    return (middle + expert_mix).astype(jnp.bfloat16)


def solution(mesh):
    placed = (
        P(("node", "ep"), None, None),
        P(None, "node"),
        P(None, "node"),
        P(None, "node"),
        P(),
        P(),
        P("ep", None, "node"),
        P("ep", "node", None),
        P(("node", "ep"), None, None),
    )
    return jax.shard_map(
        shards, mesh=mesh, in_specs=placed, out_specs=P(("node", "ep"), None, None), check_vma=False
    )
```

```python
import math

import jax
import jax.numpy as jnp
from jax import lax
from jax.sharding import PartitionSpec as P

D = 1280
HEADS = 16
CAP = 24
MOE_CHUNKS = 2


def layer_norm(values):
    center = values - jnp.mean(values, axis=-1, keepdims=True)
    spread = jnp.mean(center * center, axis=-1, keepdims=True)
    return center * lax.rsqrt(spread + 1e-06)


def slot_table(chosen, num_experts):
    onehot = (chosen[..., None] == jnp.arange(num_experts, dtype=jnp.int32)).astype(jnp.int32)
    before = jnp.cumsum(onehot, axis=1) - onehot
    return jnp.sum(before * onehot, axis=-1)


def shards(images, w_query, w_key, w_value, w_output, router, w_in, w_out, routes):
    local_images, tokens_dev, width = images.shape
    head_size = D // HEADS
    local_heads = w_query.shape[1] // head_size
    node_count = lax.axis_size("node")
    column_count = lax.axis_size("ep")
    num_experts = router.shape[1]
    local_experts = w_in.shape[0]
    slot_count = local_images * CAP
    inputs = images.astype(jnp.float32)
    normed = layer_norm(inputs).astype(jnp.bfloat16)
    node_index = lax.axis_index("node")
    ahead = [(i, (i + 1) % node_count) for i in range(node_count)]
    behind = [(i, (i - 1) % node_count) for i in range(node_count)]
    split = width // 2
    from_behind = lax.ppermute(normed, "node", ahead)
    from_ahead = lax.ppermute(normed, "node", behind)
    far = jnp.concatenate(
        [
            lax.ppermute(from_behind[..., :split], "node", ahead),
            lax.ppermute(from_ahead[..., split:], "node", behind),
        ],
        axis=-1,
    )
    shard_rows = jnp.concatenate([normed, from_ahead, far, from_behind], axis=0)
    number = shard_rows.shape[0]
    columns = w_query.shape[1]
    joined = jnp.einsum(
        "ctd,de->cet",
        shard_rows,
        jnp.concatenate([w_query, w_key, w_value], axis=1),
        preferred_element_type=jnp.float32,
    ).astype(jnp.bfloat16)
    queries = joined[:, :columns]
    projected_keys = joined[:, columns:2 * columns]
    projected_values = joined[:, 2 * columns:]
    query_heads = queries.reshape(number, local_heads, head_size, tokens_dev)
    key_heads = projected_keys.reshape(number, local_heads, head_size, tokens_dev)
    value_heads = projected_values.reshape(number, local_heads, head_size, tokens_dev)
    scores = jnp.einsum(
        "chdq,chdk->chqk", query_heads, key_heads, preferred_element_type=jnp.float32
    ) / math.sqrt(head_size)
    weights = jax.nn.softmax(scores, axis=-1).astype(jnp.bfloat16)
    mixture = jnp.einsum(
        "chqk,chdk->cqhd", weights, value_heads, preferred_element_type=jnp.float32
    ).astype(jnp.bfloat16)
    head_results = jnp.roll(mixture.reshape(number, tokens_dev, local_heads * head_size), node_index, axis=0)
    exchanged = lax.all_to_all(head_results, "node", split_axis=0, concat_axis=0, tiled=True)
    attention = jnp.einsum(
        "gtd,gde->te",
        exchanged,
        w_output.reshape(node_count, local_heads * head_size, width),
        preferred_element_type=jnp.float32,
    ).reshape(local_images, tokens_dev, width)
    middle = inputs + attention
    normed_second = layer_norm(middle).astype(jnp.bfloat16)
    logits = jnp.einsum("itd,de->ite", normed_second, router, preferred_element_type=jnp.float32)
    chosen_mask = routes[..., None] == jnp.arange(num_experts, dtype=jnp.int32)
    chosen_logit = jnp.sum(jnp.where(chosen_mask, logits[:, :, None, :], jnp.float32(0.0)), axis=-1)
    gate_values = jax.nn.sigmoid(chosen_logit)
    flat_routes = routes.reshape(local_images, 2 * tokens_dev)
    slot_index = slot_table(flat_routes, num_experts)
    image_base = jnp.arange(local_images, dtype=jnp.int32)[:, None] * CAP
    position = (flat_routes * slot_count + image_base + slot_index).reshape(-1)
    token_count = local_images * tokens_dev
    token_slots = position.reshape(token_count, 2)
    slot_ids = jnp.arange(num_experts * slot_count, dtype=jnp.int32)
    token_rows = normed_second.reshape(token_count, width)
    hits = (token_slots[None, :, 0] == slot_ids[:, None]) | (token_slots[None, :, 1] == slot_ids[:, None])
    gathered = jnp.dot(
        hits.astype(jnp.bfloat16), token_rows, preferred_element_type=jnp.float32
    ).astype(jnp.bfloat16)
    outgoing = gathered.reshape(column_count, local_experts, slot_count, width)
    chunk = slot_count // MOE_CHUNKS
    pieces = []
    for part in range(MOE_CHUNKS):
        sent = outgoing[:, :, part * chunk:(part + 1) * chunk, :]
        block = lax.all_to_all(sent, "ep", split_axis=0, concat_axis=0, tiled=True).reshape(-1, width)
        half = block.shape[0] // 2
        came_behind = lax.ppermute(block, "node", ahead)
        came_ahead = lax.ppermute(block, "node", behind)
        came_far = jnp.concatenate(
            [
                lax.ppermute(came_behind[:half], "node", ahead),
                lax.ppermute(came_ahead[half:], "node", behind),
            ],
            axis=0,
        )
        rows = jnp.concatenate([block, came_ahead, came_far, came_behind], axis=0)
        pre_act = jnp.dot(rows, w_in[0], preferred_element_type=jnp.float32)
        hidden = jax.nn.gelu(pre_act, approximate=True).astype(jnp.bfloat16)
        partial_sum = jnp.dot(hidden, w_out[0], preferred_element_type=jnp.float32).astype(jnp.bfloat16)
        own_part, next_part, far_part, prev_part = jnp.split(partial_sum, node_count, axis=0)
        got_low = lax.ppermute(far_part[:half], "node", ahead).astype(jnp.float32)
        got_high = lax.ppermute(far_part[half:], "node", behind).astype(jnp.float32)
        to_next = jnp.concatenate(
            [next_part[:half].astype(jnp.float32) + got_low, next_part[half:].astype(jnp.float32)], axis=0
        )
        to_prev = jnp.concatenate(
            [prev_part[:half].astype(jnp.float32), prev_part[half:].astype(jnp.float32) + got_high], axis=0
        )
        back_behind = lax.ppermute(to_next.astype(jnp.bfloat16), "node", ahead)
        back_ahead = lax.ppermute(to_prev.astype(jnp.bfloat16), "node", behind)
        summed = (
            own_part.astype(jnp.float32) + back_behind.astype(jnp.float32) + back_ahead.astype(jnp.float32)
        ).astype(jnp.bfloat16)
        summed = summed.reshape(column_count, local_experts, chunk, width)
        pieces.append(lax.all_to_all(summed, "ep", split_axis=0, concat_axis=0, tiled=True))
    expert_result = jnp.concatenate(pieces, axis=2)
    result_rows = expert_result.reshape(num_experts * slot_count, width)
    flat_gates = gate_values.reshape(token_count, 2)
    combine = jnp.where(token_slots[:, 0:1] == slot_ids[None, :], flat_gates[:, 0:1], jnp.float32(0.0)) + jnp.where(
        token_slots[:, 1:2] == slot_ids[None, :], flat_gates[:, 1:2], jnp.float32(0.0)
    )
    expert_mix = jnp.dot(
        combine, result_rows.astype(jnp.float32), precision=lax.Precision.HIGHEST,
        preferred_element_type=jnp.float32,
    ).reshape(local_images, tokens_dev, width)
    return (middle + expert_mix).astype(jnp.bfloat16)


def solution(mesh):
    placed = (
        P(("node", "ep"), None, None),
        P(None, "node"),
        P(None, "node"),
        P(None, "node"),
        P(),
        P(),
        P("ep", None, "node"),
        P("ep", "node", None),
        P(("node", "ep"), None, None),
    )
    return jax.shard_map(
        shards, mesh=mesh, in_specs=placed, out_specs=P(("node", "ep"), None, None), check_vma=False
    )
```

```python
import math

import jax
import jax.numpy as jnp
from jax import lax
from jax.sharding import PartitionSpec as P

D = 1280
HEADS = 16
CAP = 24
MOE_CHUNKS = 2


def layer_norm(values):
    center = values - jnp.mean(values, axis=-1, keepdims=True)
    spread = jnp.mean(center * center, axis=-1, keepdims=True)
    return center * lax.rsqrt(spread + 1e-06)


def slot_table(chosen, num_experts):
    onehot = (chosen[..., None] == jnp.arange(num_experts, dtype=jnp.int32)).astype(jnp.int32)
    before = jnp.cumsum(onehot, axis=1) - onehot
    return jnp.sum(before * onehot, axis=-1)


def shards(images, w_query, w_key, w_value, w_output, router, w_in, w_out, routes):
    local_images, tokens_dev, width = images.shape
    head_size = D // HEADS
    local_heads = w_query.shape[1] // head_size
    node_count = lax.axis_size("node")
    column_count = lax.axis_size("ep")
    num_experts = router.shape[1]
    local_experts = w_in.shape[0]
    slot_count = local_images * CAP
    inputs = images.astype(jnp.float32)
    normed = layer_norm(inputs).astype(jnp.bfloat16)
    node_index = lax.axis_index("node")
    ahead = [(i, (i + 1) % node_count) for i in range(node_count)]
    behind = [(i, (i - 1) % node_count) for i in range(node_count)]
    split = width // 2
    from_behind = lax.ppermute(normed, "node", ahead)
    from_ahead = lax.ppermute(normed, "node", behind)
    split = 128
    far = jnp.concatenate(
        [
            lax.ppermute(from_behind[:, :split], "node", ahead),
            lax.ppermute(from_ahead[:, split:], "node", behind),
        ],
        axis=1,
    )
    shard_rows = jnp.concatenate([normed, from_ahead, far, from_behind], axis=0)
    number = shard_rows.shape[0]
    columns = w_query.shape[1]
    joined = jnp.einsum(
        "ctd,de->cet",
        shard_rows,
        jnp.concatenate([w_query, w_key, w_value], axis=1),
        preferred_element_type=jnp.float32,
    ).astype(jnp.bfloat16)
    queries = joined[:, :columns]
    projected_keys = joined[:, columns:2 * columns]
    projected_values = joined[:, 2 * columns:]
    query_heads = queries.reshape(number, local_heads, head_size, tokens_dev)
    key_heads = projected_keys.reshape(number, local_heads, head_size, tokens_dev)
    value_heads = projected_values.reshape(number, local_heads, head_size, tokens_dev)
    scores = jnp.einsum(
        "chdq,chdk->chqk", query_heads, key_heads, preferred_element_type=jnp.float32
    ) / math.sqrt(head_size)
    weights = jax.nn.softmax(scores, axis=-1).astype(jnp.bfloat16)
    mixture = jnp.einsum(
        "chqk,chdk->cqhd", weights, value_heads, preferred_element_type=jnp.float32
    ).astype(jnp.bfloat16)
    head_results = jnp.roll(mixture.reshape(number, tokens_dev, local_heads * head_size), node_index, axis=0)
    exchanged = lax.all_to_all(head_results, "node", split_axis=0, concat_axis=0, tiled=True)
    attention = jnp.einsum(
        "gtd,gde->te",
        exchanged,
        w_output.reshape(node_count, local_heads * head_size, width),
        preferred_element_type=jnp.float32,
    ).reshape(local_images, tokens_dev, width)
    middle = inputs + attention
    normed_second = layer_norm(middle).astype(jnp.bfloat16)
    logits = jnp.einsum("itd,de->ite", normed_second, router, preferred_element_type=jnp.float32)
    chosen_mask = routes[..., None] == jnp.arange(num_experts, dtype=jnp.int32)
    chosen_logit = jnp.sum(jnp.where(chosen_mask, logits[:, :, None, :], jnp.float32(0.0)), axis=-1)
    gate_values = jax.nn.sigmoid(chosen_logit)
    flat_routes = routes.reshape(local_images, 2 * tokens_dev)
    slot_index = slot_table(flat_routes, num_experts)
    image_base = jnp.arange(local_images, dtype=jnp.int32)[:, None] * CAP
    position = (flat_routes * slot_count + image_base + slot_index).reshape(-1)
    token_count = local_images * tokens_dev
    token_slots = position.reshape(token_count, 2)
    slot_ids = jnp.arange(num_experts * slot_count, dtype=jnp.int32)
    token_rows = normed_second.reshape(token_count, width)
    hits = (token_slots[None, :, 0] == slot_ids[:, None]) | (token_slots[None, :, 1] == slot_ids[:, None])
    gathered = jnp.dot(
        hits.astype(jnp.bfloat16), token_rows, preferred_element_type=jnp.float32
    ).astype(jnp.bfloat16)
    outgoing = gathered.reshape(column_count, local_experts, slot_count, width)
    chunk = slot_count // MOE_CHUNKS
    pieces = []
    for part in range(MOE_CHUNKS):
        sent = outgoing[:, :, part * chunk:(part + 1) * chunk, :]
        block = lax.all_to_all(sent, "ep", split_axis=0, concat_axis=0, tiled=True).reshape(-1, width)
        half = block.shape[0] // 2
        came_behind = lax.ppermute(block, "node", ahead)
        came_ahead = lax.ppermute(block, "node", behind)
        came_far = jnp.concatenate(
            [
                lax.ppermute(came_behind[:half], "node", ahead),
                lax.ppermute(came_ahead[half:], "node", behind),
            ],
            axis=0,
        )
        rows = jnp.concatenate([block, came_ahead, came_far, came_behind], axis=0)
        pre_act = jnp.dot(rows, w_in[0], preferred_element_type=jnp.float32)
        hidden = jax.nn.gelu(pre_act, approximate=True).astype(jnp.bfloat16)
        partial_sum = jnp.dot(hidden, w_out[0], preferred_element_type=jnp.float32).astype(jnp.bfloat16)
        own_part, next_part, far_part, prev_part = jnp.split(partial_sum, node_count, axis=0)
        got_low = lax.ppermute(far_part[:half], "node", ahead).astype(jnp.float32)
        got_high = lax.ppermute(far_part[half:], "node", behind).astype(jnp.float32)
        to_next = jnp.concatenate(
            [next_part[:half].astype(jnp.float32) + got_low, next_part[half:].astype(jnp.float32)], axis=0
        )
        to_prev = jnp.concatenate(
            [prev_part[:half].astype(jnp.float32), prev_part[half:].astype(jnp.float32) + got_high], axis=0
        )
        back_behind = lax.ppermute(to_next.astype(jnp.bfloat16), "node", ahead)
        back_ahead = lax.ppermute(to_prev.astype(jnp.bfloat16), "node", behind)
        summed = (
            own_part.astype(jnp.float32) + back_behind.astype(jnp.float32) + back_ahead.astype(jnp.float32)
        ).astype(jnp.bfloat16)
        summed = summed.reshape(column_count, local_experts, chunk, width)
        pieces.append(lax.all_to_all(summed, "ep", split_axis=0, concat_axis=0, tiled=True))
    expert_result = jnp.concatenate(pieces, axis=2)
    result_rows = expert_result.reshape(num_experts * slot_count, width)
    flat_gates = gate_values.reshape(token_count, 2)
    combine = jnp.where(token_slots[:, 0:1] == slot_ids[None, :], flat_gates[:, 0:1], jnp.float32(0.0)) + jnp.where(
        token_slots[:, 1:2] == slot_ids[None, :], flat_gates[:, 1:2], jnp.float32(0.0)
    )
    expert_mix = jnp.dot(
        combine, result_rows.astype(jnp.float32), precision=lax.Precision.HIGHEST,
        preferred_element_type=jnp.float32,
    ).reshape(local_images, tokens_dev, width)
    return (middle + expert_mix).astype(jnp.bfloat16)


def solution(mesh):
    placed = (
        P(("node", "ep"), None, None),
        P(None, "node"),
        P(None, "node"),
        P(None, "node"),
        P(),
        P(),
        P("ep", None, "node"),
        P("ep", "node", None),
        P(("node", "ep"), None, None),
    )
    return jax.shard_map(
        shards, mesh=mesh, in_specs=placed, out_specs=P(("node", "ep"), None, None), check_vma=False
    )
```

```python
import math

import jax
import jax.numpy as jnp
from jax import lax
from jax.sharding import PartitionSpec as P

D = 1280
HEADS = 16
CAP = 24
MOE_CHUNKS = 2


def layer_norm(values):
    center = values - jnp.mean(values, axis=-1, keepdims=True)
    spread = jnp.mean(center * center, axis=-1, keepdims=True)
    return center * lax.rsqrt(spread + 1e-06)


def slot_table(chosen, num_experts):
    onehot = (chosen[..., None] == jnp.arange(num_experts, dtype=jnp.int32)).astype(jnp.int32)
    before = jnp.cumsum(onehot, axis=1) - onehot
    return jnp.sum(before * onehot, axis=-1)


def shards(images, w_query, w_key, w_value, w_output, router, w_in, w_out, routes):
    local_images, tokens_dev, width = images.shape
    head_size = D // HEADS
    local_heads = w_query.shape[1] // head_size
    node_count = lax.axis_size("node")
    column_count = lax.axis_size("ep")
    num_experts = router.shape[1]
    local_experts = w_in.shape[0]
    slot_count = local_images * CAP
    inputs = images.astype(jnp.float32)
    normed = layer_norm(inputs).astype(jnp.bfloat16)
    node_index = lax.axis_index("node")
    ahead = [(i, (i + 1) % node_count) for i in range(node_count)]
    behind = [(i, (i - 1) % node_count) for i in range(node_count)]
    split = width // 2
    from_behind = lax.ppermute(normed, "node", ahead)
    from_ahead = lax.ppermute(normed, "node", behind)
    far = jnp.concatenate(
        [
            lax.ppermute(from_behind[..., :split], "node", ahead),
            lax.ppermute(from_ahead[..., split:], "node", behind),
        ],
        axis=-1,
    )
    shard_rows = jnp.concatenate([normed, from_ahead, far, from_behind], axis=0)
    number = shard_rows.shape[0]
    columns = w_query.shape[1]
    joined = jnp.einsum(
        "ctd,de->cet",
        shard_rows,
        jnp.concatenate([w_query, w_key, w_value], axis=1),
        preferred_element_type=jnp.float32,
    ).astype(jnp.bfloat16)
    queries = joined[:, :columns]
    projected_keys = joined[:, columns:2 * columns]
    projected_values = joined[:, 2 * columns:]
    query_heads = queries.reshape(number, local_heads, head_size, tokens_dev)
    key_heads = projected_keys.reshape(number, local_heads, head_size, tokens_dev)
    value_heads = projected_values.reshape(number, local_heads, head_size, tokens_dev)
    scores = jnp.einsum(
        "chdq,chdk->chqk", query_heads, key_heads, preferred_element_type=jnp.float32
    ) / math.sqrt(head_size)
    weights = jax.nn.softmax(scores, axis=-1).astype(jnp.bfloat16)
    mixture = jnp.einsum(
        "chqk,chdk->cqhd", weights, value_heads, preferred_element_type=jnp.float32
    ).astype(jnp.bfloat16)
    head_results = jnp.roll(mixture.reshape(number, tokens_dev, local_heads * head_size), node_index, axis=0)
    exchanged = lax.all_to_all(head_results, "node", split_axis=0, concat_axis=0, tiled=True)
    attention = jnp.einsum(
        "gtd,gde->te",
        exchanged,
        w_output.reshape(node_count, local_heads * head_size, width),
        preferred_element_type=jnp.float32,
    ).reshape(local_images, tokens_dev, width)
    middle = inputs + attention
    normed_second = layer_norm(middle).astype(jnp.bfloat16)
    logits = jnp.einsum("itd,de->ite", normed_second, router, preferred_element_type=jnp.float32)
    chosen_mask = routes[..., None] == jnp.arange(num_experts, dtype=jnp.int32)
    chosen_logit = jnp.sum(jnp.where(chosen_mask, logits[:, :, None, :], jnp.float32(0.0)), axis=-1)
    gate_values = jax.nn.sigmoid(chosen_logit)
    flat_routes = routes.reshape(local_images, 2 * tokens_dev)
    slot_index = slot_table(flat_routes, num_experts)
    image_base = jnp.arange(local_images, dtype=jnp.int32)[:, None] * CAP
    position = (flat_routes * slot_count + image_base + slot_index).reshape(-1)
    token_count = local_images * tokens_dev
    token_slots = position.reshape(token_count, 2)
    slot_ids = jnp.arange(num_experts * slot_count, dtype=jnp.int32)
    token_rows = normed_second.reshape(token_count, width)
    hits = (token_slots[None, :, 0] == slot_ids[:, None]) | (token_slots[None, :, 1] == slot_ids[:, None])
    gathered = jnp.dot(
        hits.astype(jnp.bfloat16), token_rows, preferred_element_type=jnp.float32
    ).astype(jnp.bfloat16)
    outgoing = gathered.reshape(column_count, local_experts, slot_count, width)
    chunk = slot_count // MOE_CHUNKS
    pieces = []
    for part in range(MOE_CHUNKS):
        sent = outgoing[:, :, part * chunk:(part + 1) * chunk, :]
        block = lax.all_to_all(sent, "ep", split_axis=0, concat_axis=0, tiled=True).reshape(-1, width)
        half = block.shape[0] // 2
        came_behind = lax.ppermute(block, "node", ahead)
        came_ahead = lax.ppermute(block, "node", behind)
        came_far = jnp.concatenate(
            [
                lax.ppermute(came_behind[:half], "node", ahead),
                lax.ppermute(came_ahead[half:], "node", behind),
            ],
            axis=0,
        )
        rows = jnp.concatenate([block, came_ahead, came_far, came_behind], axis=0)
        pre_act = jnp.dot(rows, w_in[0], preferred_element_type=jnp.float32)
        hidden = jax.nn.gelu(pre_act, approximate=True).astype(jnp.bfloat16)
        partial_sum = jnp.dot(hidden, w_out[0], preferred_element_type=jnp.float32).astype(jnp.bfloat16)
        own_part, next_part, far_part, prev_part = jnp.split(partial_sum, node_count, axis=0)
        got_low = lax.ppermute(far_part[:half], "node", ahead).astype(jnp.float32)
        got_high = lax.ppermute(far_part[half:], "node", behind).astype(jnp.float32)
        to_next = jnp.concatenate(
            [next_part[:half].astype(jnp.float32) + got_low, next_part[half:].astype(jnp.float32)], axis=0
        )
        to_prev = jnp.concatenate(
            [prev_part[:half].astype(jnp.float32), prev_part[half:].astype(jnp.float32) + got_high], axis=0
        )
        back_behind = lax.ppermute(to_next.astype(jnp.bfloat16), "node", ahead)
        back_ahead = lax.ppermute(to_prev.astype(jnp.bfloat16), "node", behind)
        summed = (
            own_part.astype(jnp.float32) + back_behind.astype(jnp.float32) + back_ahead.astype(jnp.float32)
        ).astype(jnp.bfloat16)
        summed = summed.reshape(column_count, local_experts, chunk, width)
        pieces.append(lax.all_to_all(summed, "ep", split_axis=0, concat_axis=0, tiled=True))
    expert_result = jnp.concatenate(pieces, axis=2)
    result_rows = expert_result.reshape(num_experts * slot_count, width)
    flat_gates = gate_values.reshape(token_count, 2)
    combine = jnp.where(token_slots[:, 0:1] == slot_ids[None, :], flat_gates[:, 0:1], jnp.float32(0.0)) + jnp.where(
        token_slots[:, 1:2] == slot_ids[None, :], flat_gates[:, 1:2], jnp.float32(0.0)
    )
    expert_mix = jnp.dot(
        combine, result_rows.astype(jnp.float32), precision=lax.Precision.HIGH,
        preferred_element_type=jnp.float32,
    ).reshape(local_images, tokens_dev, width)
    return (middle + expert_mix).astype(jnp.bfloat16)


def solution(mesh):
    placed = (
        P(("node", "ep"), None, None),
        P(None, "node"),
        P(None, "node"),
        P(None, "node"),
        P(),
        P(),
        P("ep", None, "node"),
        P("ep", "node", None),
        P(("node", "ep"), None, None),
    )
    return jax.shard_map(
        shards, mesh=mesh, in_specs=placed, out_specs=P(("node", "ep"), None, None), check_vma=False
    )
```
